1024 devices in a mesh: gy: 16 (over x_hi, y, core), gx: 64 (over x_lo, z).
Axes of the slice: x: 4 (x_hi: 2, x_lo: 2; x = x_hi * 2 + x_lo), y: 4, z: 32, core: 2. Of those that a mesh axis runs over, the one named last changes fastest.
Arguments:
- ocean_blocks: float32 [1024, 4, 8192], P('gy', None, 'gx'), may hold values from -4 to 4
- block_map: int32 [1024, 64], P('gy', 'gx'), may hold values from 0 to 4095, as said below
- velocity: float32 [2, 1024, 8192], P(None, 'gy', 'gx'), may hold values from -2 to 2
- stress: float32 [3, 1024, 8192], P(None, 'gy', 'gx'), may hold values from -3 to 3
- thickness: float32 [5, 1024, 8192], P(None, 'gy', 'gx'), may hold values from 0.05 to 5
- area: float32 [5, 1024, 8192], P(None, 'gy', 'gx'), may hold values from 0.1 to 0.2
- wind: float32 [2, 1024, 8192], P(None, 'gy', 'gx'), may hold values from -3 to 3
- air_temp: float32 [1024, 8192], P('gy', 'gx'), may hold values from -6 to 0
- ice_presence_mask: int32 [1024, 8192], P('gy', 'gx'), may hold values 0 or 1
- ocean_land_mask: int32 [1024, 8192], P('gy', 'gx'), may hold values 0 or 1
- fold_partner_column: int32 [8192], replicated, may hold values from 0 to 8191, as said below
Outputs:
- velocity_out: float32 [2, 1024, 8192], P(None, 'gy', 'gx')
- stress_out: float32 [3, 1024, 8192], P(None, 'gy', 'gx')
- thickness_out: float32 [5, 1024, 8192], P(None, 'gy', 'gx')
The draws below stay inside these ranges and needn't reach their ends.
Inputs may be any that keep to these rules, and one draw needn't show every extreme that they name: Within each latitude row of devices block_map is a permutation of 0 to 4095; value p * 64 + t names device p, row t. The slots k * 2 to (k + 1) * 2 - 1 of one device all go to one device, into rows k * 2 to (k + 1) * 2 - 1; different k of one device go to different devices. fold_partner_column[i] = (c - i) mod 8192 for one c per draw, so the table is its own inverse.
All inputs are finite; a program needn't handle non-finite values. No bound on the sum of `ice_presence_mask` or of `ocean_land_mask` on one device may be relied on, other than what follows from the above.
Results may differ from the reference program's by a relative error of at most 0.0001.
Values sent between devices are 32-bit elements; how exact they have to be, the bound alone decides.
No kernel may reach another device: no remote copies, remote signals or barrier semaphores. Data moves between devices by JAX's collectives and lax.ppermute only.
A program may use at most 32 MiB of HBM per device.

```python
import math
import jax
import jax.numpy as jnp
from jax import lax

CY = 64
CX = 128
NCAT = 5
ITERS = 4
NY = 1024
NX = 8192
N_GY = 16
N_GX = 64


def draw_block_map(key, part):
    group = max(2, CY // N_GX)
    count = CY // group

    def one_row(row_key):
        key_order, key_shift, key_inner = jax.random.split(row_key, 3)
        order = jax.random.permutation(key_order, N_GX).astype(jnp.int32)
        place = jnp.zeros((N_GX,), jnp.int32).at[order].set(jnp.arange(N_GX, dtype=jnp.int32))
        shifts = jax.random.permutation(key_shift, N_GX).astype(jnp.int32)[:count]
        inner_keys = jax.random.split(key_inner, N_GX * count)

        def inner_order(small_key):
            return jax.random.permutation(small_key, group).astype(jnp.int32)
        inner = jax.vmap(inner_order)(inner_keys).reshape(N_GX, count, group)
        dest_dev = order[(place[:, None] + shifts[None, :]) % N_GX]
        dest_row = jnp.arange(count, dtype=jnp.int32)[None, :, None] * group + inner
        value = dest_dev[:, :, None] * CY + dest_row
        return value.reshape(N_GX, CY).T
    row_keys = jax.random.split(jax.random.fold_in(key, 11), N_GY)
    rows = jax.vmap(one_row)(row_keys)
    return rows.reshape(N_GY * CY, N_GX).astype(jnp.int32)


def draw_fold_partner_column(key, part):
    offset = jax.random.randint(jax.random.fold_in(key, 5), (), 0, NX, dtype=jnp.int32)
    return ((offset - jnp.arange(NX, dtype=jnp.int32)) % NX).astype(jnp.int32)


def touch_ends(drawn, rng, least, top_value):
    spot = [jax.random.randint(jax.random.fold_in(rng, axis), (), 0, length) for axis, length in enumerate(drawn.shape)]
    widest = drawn.shape.index(max(drawn.shape))
    beside = spot[:widest] + [(spot[widest] + 1) % drawn.shape[widest]] + spot[widest + 1:]
    return drawn.at[tuple(spot)].set(least).at[tuple(beside)].set(top_value)


def block_scale(rng, extent, shards, least, largest):
    factor_of = 1.0
    for dim, shards_of in shards:
        steps = jax.random.uniform(jax.random.fold_in(jax.random.fold_in(rng, 6), dim), (shards_of,), jnp.float32, least / len(shards), largest / len(shards))
        factor_of = factor_of * jnp.repeat(jnp.exp(steps), extent[dim] // shards_of).reshape((-1,) + (1,) * (len(extent) - 1 - dim))
    return factor_of


def gaussian(own_key, dims, scale, limit, shards=(), kind=jnp.bfloat16):
    values = jax.random.normal(own_key, dims, jnp.float32) * scale
    if len(shards) > 0:
        values = block_scale(own_key, dims, shards, -0.22, 0.18) * values
    return jnp.clip(values, min=-limit, max=limit).astype(kind)


def setup_inputs(seed: int = 0) -> dict:
    arg_keys = jax.random.split(jax.random.key(seed), 12)
    ocean_blocks = gaussian(arg_keys[0], (NY, 4, NX), 1.0, 4.0, ((0, 16), (2, 64)), jnp.float32)
    block_map = draw_block_map(jax.random.fold_in(arg_keys[11], 71), 0)
    velocity = gaussian(arg_keys[2], (2, NY, NX), 0.3, 2.0, ((1, 16), (2, 64)), jnp.float32)
    stress = gaussian(arg_keys[3], (3, NY, NX), 0.5, 3.0, ((1, 16), (2, 64)), jnp.float32)
    thickness = jnp.clip(jnp.exp(math.log(5.0) - 4.6051702 * jax.random.uniform(arg_keys[4], (NCAT, NY, NX), jnp.float32) ** block_scale(arg_keys[4], (NCAT, NY, NX), ((1, 16), (2, 64)), -0.2, 0.2)), 0.05, 5.0)
    area = jnp.clip(0.1 + 0.1 * jax.random.uniform(arg_keys[5], (NCAT, NY, NX), jnp.float32) ** block_scale(arg_keys[5], (NCAT, NY, NX), ((1, 16), (2, 64)), -0.2, 0.2), 0.1, 0.2)
    wind = gaussian(arg_keys[6], (2, NY, NX), 0.5, 3.0, ((1, 16), (2, 64)), jnp.float32)
    air_temp = jnp.clip(-6.0 + 6.0 * jax.random.uniform(arg_keys[7], (NY, NX), jnp.float32) ** block_scale(arg_keys[7], (NY, NX), ((0, 16), (1, 64)), -0.2, 0.2), -6.0, 0.0)
    ice_presence_mask = touch_ends((jax.random.randint(arg_keys[8], (NY, NX), 0, 4) < 3).astype(jnp.int32), jax.random.fold_in(arg_keys[8], 1), 0, 1)
    ocean_land_mask = touch_ends((jax.random.randint(arg_keys[9], (NY, NX), 0, 10) < 9).astype(jnp.int32), jax.random.fold_in(arg_keys[9], 1), 0, 1)
    fold_partner_column = draw_fold_partner_column(jax.random.fold_in(arg_keys[11], 71), 0)
    return {"ocean_blocks": ocean_blocks, "block_map": block_map, "velocity": velocity, "stress": stress, "thickness": thickness, "area": area, "wind": wind, "air_temp": air_temp, "ice_presence_mask": ice_presence_mask, "ocean_land_mask": ocean_land_mask, "fold_partner_column": fold_partner_column}


RELAX = 0.5
ECC2 = 4.0
DMIN2 = 0.01
PSTAR = 1.0
CSTAR = 5.0
DTE = 0.3
DRAG = 1.0
FCOR = 0.5
KAPPA = 0.5
GAMMA = 0.3
DTT = 0.5
SREF = 34.0

def regroup(ocean_blocks, block_map):
    source = ocean_blocks.reshape(N_GY, CY, 4, N_GX, CX).transpose(0, 3, 1, 2, 4).reshape(N_GY, N_GX * CY, 4, CX)
    target = block_map.reshape(N_GY, CY, N_GX).transpose(0, 2, 1).reshape(N_GY, N_GX * CY)
    row_select = jnp.arange(N_GY, dtype=jnp.int32)[:, None]
    placed = jnp.zeros_like(source).at[row_select, target].set(source)
    return placed.reshape(N_GY, N_GX, CY, 4, CX).transpose(0, 2, 3, 1, 4).reshape(NY, 4, NX)

def global_rim_field(field, signs, fold_partner_column):
    columns = jnp.arange(-1, NX + 1, dtype=jnp.int32) % NX
    middle = jnp.take(field, columns, axis=2)
    north = jnp.take(field[:, NY - 1:NY, :], fold_partner_column[columns], axis=2) * signs
    south = jnp.zeros_like(north)
    return jnp.concatenate([south, middle, north], axis=1)

def compute_strain_rates(u_pad, v_pad):
    strain_rate_east = (u_pad[1:-1, 2:] - u_pad[1:-1, :-2]) * 0.5
    strain_rate_north = (v_pad[2:, 1:-1] - v_pad[:-2, 1:-1]) * 0.5
    strain_rate_shear = (u_pad[2:, 1:-1] - u_pad[:-2, 1:-1] + (v_pad[1:-1, 2:] - v_pad[1:-1, :-2])) * 0.25
    return (strain_rate_east, strain_rate_north, strain_rate_shear)

def stress_update(old, strain_rate_east, strain_rate_north, strain_rate_shear, strength):
    divergence = strain_rate_east + strain_rate_north
    tension = strain_rate_east - strain_rate_north
    shear = 2.0 * strain_rate_shear
    delta = jnp.sqrt(divergence * divergence + (tension * tension + shear * shear) / ECC2 + DMIN2)
    zeta = strength / delta
    first = (old[0] + RELAX * (zeta * divergence - strength)) / (1.0 + RELAX)
    second = (old[1] + RELAX * zeta * tension / ECC2) / (1.0 + RELAX)
    third = (old[2] + RELAX * zeta * shear / (2.0 * ECC2)) / (1.0 + RELAX)
    return jnp.stack([first, second, third])

def stress_force(padded):
    normal_x = (padded[0] + padded[1]) * 0.5
    normal_y = (padded[0] - padded[1]) * 0.5
    shear = padded[2]
    eastward_force = (normal_x[1:-1, 2:] - normal_x[1:-1, :-2]) * 0.5 + (shear[2:, 1:-1] - shear[:-2, 1:-1]) * 0.5
    northward_force = (shear[1:-1, 2:] - shear[1:-1, :-2]) * 0.5 + (normal_y[2:, 1:-1] - normal_y[:-2, 1:-1]) * 0.5
    return (eastward_force, northward_force)

def momentum_solve(velocity, eastward_force, northward_force, wind, ocean_current_east, ocean_current_north, ice_mass_per_area, coriolis_parameter, velocity_mask):
    east = velocity[0]
    north = velocity[1]
    implicit_denominator = ice_mass_per_area + DTE * DRAG
    right_side_east = east * ice_mass_per_area + DTE * (eastward_force + wind[0] + DRAG * ocean_current_east + ice_mass_per_area * coriolis_parameter * north)
    right_side_north = north * ice_mass_per_area + DTE * (northward_force + wind[1] + DRAG * ocean_current_north - ice_mass_per_area * coriolis_parameter * east)
    return jnp.stack([velocity_mask * right_side_east / implicit_denominator, velocity_mask * right_side_north / implicit_denominator])

def column_growth(thickness, velocity, ocean_temp, ocean_salt, ocean_current_east, ocean_current_north, air_temp, omask):
    freeze = -0.054 * (SREF + ocean_salt)
    rel_east = velocity[0] - ocean_current_east
    rel_north = velocity[1] - ocean_current_north
    speed = jnp.sqrt(rel_east * rel_east + rel_north * rel_north + 0.01)
    melt = GAMMA * (ocean_temp - freeze) * speed
    growth = KAPPA * (freeze - air_temp) / (thickness + 0.1)
    return omask * jnp.maximum(thickness + DTT * (growth - melt), 0.0)

def reference(ocean_blocks, block_map, velocity, stress, thickness, area, wind, air_temp, ice_presence_mask, ocean_land_mask, fold_partner_column):
    ocean = regroup(ocean_blocks, block_map)
    ocean_temp = ocean[:, 0, :]
    ocean_salt = ocean[:, 1, :]
    ocean_current_east = ocean[:, 2, :]
    ocean_current_north = ocean[:, 3, :]
    hsum = lax.optimization_barrier(jnp.sum(area * thickness, axis=0))
    conc = lax.optimization_barrier(jnp.sum(area, axis=0))
    strength = PSTAR * hsum * jnp.exp(-CSTAR * (1.0 - conc))
    ice_mass_per_area = hsum + 0.2
    row_float = jnp.arange(NY, dtype=jnp.int32).astype(jnp.float32)
    coriolis_parameter = (FCOR * (row_float + 0.5) / float(NY))[:, None]
    velocity_mask = (ice_presence_mask * ocean_land_mask).astype(jnp.float32)
    omask = ocean_land_mask.astype(jnp.float32)
    velocity_fold_sign = jnp.array([-1.0, -1.0], dtype=jnp.float32).reshape(2, 1, 1)
    ssign = jnp.ones((3, 1, 1), dtype=jnp.float32)
    for step in range(ITERS):
        velocity_padded = global_rim_field(velocity, velocity_fold_sign, fold_partner_column)
        strain_rate_east, strain_rate_north, strain_rate_shear = compute_strain_rates(velocity_padded[0], velocity_padded[1])
        stress = stress_update(stress, strain_rate_east, strain_rate_north, strain_rate_shear, strength)
        spad = global_rim_field(stress, ssign, fold_partner_column)
        eastward_force, northward_force = stress_force(spad)
        velocity = momentum_solve(velocity, eastward_force, northward_force, wind, ocean_current_east, ocean_current_north, ice_mass_per_area, coriolis_parameter, velocity_mask)
    thickness_out = column_growth(thickness, velocity, ocean_temp, ocean_salt, ocean_current_east, ocean_current_north, air_temp, omask)
    return (velocity, stress, thickness_out)
```

```python
import jax
import jax.numpy as jnp
from jax import lax
from jax.sharding import PartitionSpec as P

ITERS = 4


RELAX = 0.5
ECC2 = 4.0
DMIN2 = 0.01
PSTAR = 1.0
CSTAR = 5.0
DTE = 0.3
DRAG = 1.0
FCOR = 0.5
KAPPA = 0.5
GAMMA = 0.3
DTT = 0.5
SREF = 34.0


def shift_pairs(count, step, cyclic):
    pairs = [(i, i + step) for i in range(count) if 0 <= i + step < count]
    if cyclic:
        pairs = [(i, (i + step) % count) for i in range(count)]
    return pairs


def regroup_local(ocean_blocks, block_map):
    rows, fields, cols = ocean_blocks.shape
    peers = lax.axis_size("gx")
    group = max(2, rows // peers)
    count = rows // group
    target = block_map[:, 0]
    dest_dev = target[::group] // rows
    dest_row = (target % rows).reshape(count, group)
    chosen = dest_dev[None, :] == jnp.arange(peers, dtype=jnp.int32)[:, None]
    blocks = ocean_blocks.reshape(count, group * fields * cols)
    outgoing = jnp.dot(
        chosen.astype(jnp.float32),
        blocks,
        precision=lax.Precision.HIGHEST,
        preferred_element_type=jnp.float32,
    )
    labels = jnp.sum(jnp.where(chosen[:, :, None], dest_row[None, :, :] + 1, 0), axis=1) - 1
    packed = jnp.concatenate([outgoing, labels.astype(jnp.float32)], axis=1)
    arrived = lax.all_to_all(packed, "gx", split_axis=0, concat_axis=0, tiled=True)
    flat = arrived[:, : group * fields * cols].reshape(peers * group, fields * cols)
    arrived_rows = arrived[:, group * fields * cols :].astype(jnp.int32)
    picks = (
        arrived_rows.reshape(-1)[None, :] == jnp.arange(rows, dtype=jnp.int32)[:, None]
    ).astype(jnp.float32)
    local = jnp.dot(
        picks, flat, precision=lax.Precision.HIGHEST, preferred_element_type=jnp.float32
    )
    return local.reshape(rows, fields, cols)


def fold_row(top, fold_start, fold_rest):
    peers = lax.axis_size("gx")
    cols = top.shape[-1]
    low = 8 if peers % 8 == 0 else 1
    a = fold_start // low
    b = fold_start % low

    def reflect(aa):
        return lambda t: lax.ppermute(
            t, "gx", [(e, (low * aa - e) % peers) for e in range(peers)]
        )

    def shift(bb):
        def run(y):
            near = lax.ppermute(y, "gx", [(e, (e + bb) % peers) for e in range(peers)])
            far = lax.ppermute(y, "gx", [(e, (e + bb - 1) % peers) for e in range(peers)])
            return near, far

        return run

    mirrored = lax.switch(a, [reflect(aa) for aa in range(peers // low)], top)
    near, far = lax.switch(b, [shift(bb) for bb in range(low)], mirrored)
    both = jnp.concatenate([far, near], axis=-1)
    picked = lax.dynamic_slice_in_dim(both, fold_rest + 1, cols, axis=-1)
    return jnp.flip(picked, axis=-1)


def attach_rim_halo(field, signs, fold_start, fold_rest):
    ny = lax.axis_size("gy")
    nx = lax.axis_size("gx")
    south = lax.ppermute(field[:, -1:, :], "gy", shift_pairs(ny, 1, False))
    north = lax.ppermute(field[:, :1, :], "gy", shift_pairs(ny, -1, False))
    west = lax.ppermute(field[:, :, -1:], "gx", shift_pairs(nx, 1, True))
    east = lax.ppermute(field[:, :, :1], "gx", shift_pairs(nx, -1, True))
    folded = fold_row(field[:, -1, :], fold_start, fold_rest)[:, None, :] * signs
    north = jnp.where(lax.axis_index("gy") == ny - 1, folded, north)
    rows = jnp.concatenate([south, field, north], axis=1)
    corner = jnp.zeros_like(rows[:, :, :1])
    west = jnp.concatenate([corner[:, :1], west, corner[:, :1]], axis=1)
    east = jnp.concatenate([corner[:, :1], east, corner[:, :1]], axis=1)
    return jnp.concatenate([west, rows, east], axis=2)


def compute_strain_rates(u_pad, v_pad):
    strain_rate_east = (u_pad[1:-1, 2:] - u_pad[1:-1, :-2]) * 0.5
    strain_rate_north = (v_pad[2:, 1:-1] - v_pad[:-2, 1:-1]) * 0.5
    strain_rate_shear = (
        u_pad[2:, 1:-1] - u_pad[:-2, 1:-1] + (v_pad[1:-1, 2:] - v_pad[1:-1, :-2])
    ) * 0.25
    return (strain_rate_east, strain_rate_north, strain_rate_shear)


def stress_update(old, strain_rate_east, strain_rate_north, strain_rate_shear, strength):
    divergence = strain_rate_east + strain_rate_north
    tension = strain_rate_east - strain_rate_north
    shear = 2.0 * strain_rate_shear
    delta = jnp.sqrt(divergence * divergence + (tension * tension + shear * shear) / ECC2 + DMIN2)
    zeta = strength / delta
    first = (old[0] + RELAX * (zeta * divergence - strength)) / (1.0 + RELAX)
    second = (old[1] + RELAX * zeta * tension / ECC2) / (1.0 + RELAX)
    third = (old[2] + RELAX * zeta * shear / (2.0 * ECC2)) / (1.0 + RELAX)
    return jnp.stack([first, second, third])


def stress_force(padded):
    normal_x = (padded[0] + padded[1]) * 0.5
    normal_y = (padded[0] - padded[1]) * 0.5
    shear = padded[2]
    eastward_force = (normal_x[1:-1, 2:] - normal_x[1:-1, :-2]) * 0.5 + (
        shear[2:, 1:-1] - shear[:-2, 1:-1]
    ) * 0.5
    northward_force = (shear[1:-1, 2:] - shear[1:-1, :-2]) * 0.5 + (
        normal_y[2:, 1:-1] - normal_y[:-2, 1:-1]
    ) * 0.5
    return (eastward_force, northward_force)


def momentum_solve(
    velocity,
    eastward_force,
    northward_force,
    wind,
    ocean_current_east,
    ocean_current_north,
    ice_mass_per_area,
    coriolis_parameter,
    velocity_mask,
):
    east = velocity[0]
    north = velocity[1]
    implicit_denominator = ice_mass_per_area + DTE * DRAG
    right_side_east = east * ice_mass_per_area + DTE * (
        eastward_force
        + wind[0]
        + DRAG * ocean_current_east
        + ice_mass_per_area * coriolis_parameter * north
    )
    right_side_north = north * ice_mass_per_area + DTE * (
        northward_force
        + wind[1]
        + DRAG * ocean_current_north
        - ice_mass_per_area * coriolis_parameter * east
    )
    return jnp.stack(
        [
            velocity_mask * right_side_east / implicit_denominator,
            velocity_mask * right_side_north / implicit_denominator,
        ]
    )


def column_growth(
    thickness,
    velocity,
    ocean_temp,
    ocean_salt,
    ocean_current_east,
    ocean_current_north,
    air_temp,
    omask,
):
    freeze = -0.054 * (SREF + ocean_salt)
    rel_east = velocity[0] - ocean_current_east
    rel_north = velocity[1] - ocean_current_north
    speed = jnp.sqrt(rel_east * rel_east + rel_north * rel_north + 0.01)
    melt = GAMMA * (ocean_temp - freeze) * speed
    growth = KAPPA * (freeze - air_temp) / (thickness + 0.1)
    return omask * jnp.maximum(thickness + DTT * (growth - melt), 0.0)


def body(
    ocean_blocks,
    block_map,
    velocity,
    stress,
    thickness,
    area,
    wind,
    air_temp,
    ice_presence_mask,
    ocean_land_mask,
    fold_partner_column,
):
    ocean = regroup_local(ocean_blocks, block_map)
    ocean_temp = ocean[:, 0, :]
    ocean_salt = ocean[:, 1, :]
    ocean_current_east = ocean[:, 2, :]
    ocean_current_north = ocean[:, 3, :]
    hsum = jnp.sum(area * thickness, axis=0)
    conc = jnp.sum(area, axis=0)
    strength = PSTAR * hsum * jnp.exp(-CSTAR * (1.0 - conc))
    ice_mass_per_area = hsum + 0.2
    rows = velocity.shape[1]
    total_rows = rows * lax.axis_size("gy")
    row_float = (lax.axis_index("gy") * rows + jnp.arange(rows, dtype=jnp.int32)).astype(
        jnp.float32
    )
    coriolis_parameter = (FCOR * (row_float + 0.5) / float(total_rows))[:, None]
    velocity_mask = (ice_presence_mask * ocean_land_mask).astype(jnp.float32)
    omask = ocean_land_mask.astype(jnp.float32)
    velocity_fold_sign = jnp.array([-1.0, -1.0], dtype=jnp.float32).reshape(2, 1, 1)
    ssign = jnp.ones((3, 1, 1), dtype=jnp.float32)
    cols = velocity.shape[2]
    fold_col = fold_partner_column[0] % (cols * lax.axis_size("gx"))
    fold_start = fold_col // cols
    fold_rest = fold_col % cols
    def subcycle(step, state):
        velocity, stress = state
        velocity_padded = attach_rim_halo(velocity, velocity_fold_sign, fold_start, fold_rest)
        strain_rate_east, strain_rate_north, strain_rate_shear = compute_strain_rates(
            velocity_padded[0], velocity_padded[1]
        )
        stress = stress_update(
            stress, strain_rate_east, strain_rate_north, strain_rate_shear, strength
        )
        spad = attach_rim_halo(stress, ssign, fold_start, fold_rest)
        eastward_force, northward_force = stress_force(spad)
        velocity = momentum_solve(
            velocity,
            eastward_force,
            northward_force,
            wind,
            ocean_current_east,
            ocean_current_north,
            ice_mass_per_area,
            coriolis_parameter,
            velocity_mask,
        )
        return velocity, stress

    velocity, stress = lax.fori_loop(0, ITERS, subcycle, (velocity, stress))
    thickness_out = column_growth(
        thickness,
        velocity,
        ocean_temp,
        ocean_salt,
        ocean_current_east,
        ocean_current_north,
        air_temp,
        omask,
    )
    return (velocity, stress, thickness_out)


def solution(mesh):
    placed = (
        P("gy", None, "gx"),
        P("gy", "gx"),
        P(None, "gy", "gx"),
        P(None, "gy", "gx"),
        P(None, "gy", "gx"),
        P(None, "gy", "gx"),
        P(None, "gy", "gx"),
        P("gy", "gx"),
        P("gy", "gx"),
        P("gy", "gx"),
        P(),
    )
    return jax.shard_map(
        body,
        mesh=mesh,
        in_specs=placed,
        out_specs=(P(None, "gy", "gx"), P(None, "gy", "gx"), P(None, "gy", "gx")),
        check_vma=False,
    )
```

```python
import jax
import jax.numpy as jnp
from jax import lax
from jax.sharding import PartitionSpec as P

ITERS = 4


RELAX = 0.5
ECC2 = 4.0
DMIN2 = 0.01
PSTAR = 1.0
CSTAR = 5.0
DTE = 0.3
DRAG = 1.0
FCOR = 0.5
KAPPA = 0.5
GAMMA = 0.3
DTT = 0.5
SREF = 34.0


def shift_pairs(count, step, cyclic):
    pairs = [(i, i + step) for i in range(count) if 0 <= i + step < count]
    if cyclic:
        pairs = [(i, (i + step) % count) for i in range(count)]
    return pairs


def regroup_local(ocean_blocks, block_map):
    rows, fields, cols = ocean_blocks.shape
    peers = lax.axis_size("gx")
    group = max(2, rows // peers)
    count = rows // group
    target = block_map[:, 0]
    dest_dev = target[::group] // rows
    dest_row = (target % rows).reshape(count, group)
    chosen = dest_dev[None, :] == jnp.arange(peers, dtype=jnp.int32)[:, None]
    blocks = ocean_blocks.reshape(count, group * fields * cols)
    outgoing = jnp.dot(
        chosen.astype(jnp.float32),
        blocks,
        precision=lax.Precision.HIGHEST,
        preferred_element_type=jnp.float32,
    )
    labels = jnp.sum(jnp.where(chosen[:, :, None], dest_row[None, :, :] + 1, 0), axis=1) - 1
    packed = jnp.concatenate([outgoing, labels.astype(jnp.float32)], axis=1)
    arrived = lax.all_to_all(packed, "gx", split_axis=0, concat_axis=0, tiled=True)
    flat = arrived[:, : group * fields * cols].reshape(peers * group, fields * cols)
    arrived_rows = arrived[:, group * fields * cols :].astype(jnp.int32)
    picks = (
        arrived_rows.reshape(-1)[None, :] == jnp.arange(rows, dtype=jnp.int32)[:, None]
    ).astype(jnp.float32)
    local = jnp.dot(
        picks, flat, precision=lax.Precision.HIGHEST, preferred_element_type=jnp.float32
    )
    return local.reshape(rows, fields, cols)


def fold_strip(top, fold_start, fold_rest, width):
    peers = lax.axis_size("gx")
    cols = top.shape[-1]
    low = 8 if peers % 8 == 0 else 1
    a = fold_start // low
    b = fold_start % low

    def reflect(aa):
        return lambda t: lax.ppermute(
            t, "gx", [(e, (low * aa - e) % peers) for e in range(peers)]
        )

    def shift(bb):
        return lambda y: tuple(
            lax.ppermute(y, "gx", [(e, (e + bb + t) % peers) for e in range(peers)])
            for t in (-2, -1, 0, 1)
        )

    mirrored = lax.switch(a, [reflect(aa) for aa in range(peers // low)], top)
    parts = lax.switch(b, [shift(bb) for bb in range(low)], mirrored)
    strip = jnp.concatenate(parts, axis=-1)
    first = 2 * cols + fold_rest - (cols - 1) - width
    window = lax.dynamic_slice_in_dim(strip, first, cols + 2 * width, axis=2)
    return jnp.flip(window, axis=(1, 2))


def exchange(stack, width, signs, fold_start, fold_rest):
    ny = lax.axis_size("gy")
    nx = lax.axis_size("gx")
    w = width

    def diag(dy, dx):
        return [
            (y * nx + x, (y + dy) * nx + (x + dx) % nx)
            for y in range(ny)
            for x in range(nx)
            if 0 <= y + dy < ny
        ]

    both = ("gy", "gx")
    south = lax.ppermute(stack[:, -w:, :], "gy", shift_pairs(ny, 1, False))
    north = lax.ppermute(stack[:, :w, :], "gy", shift_pairs(ny, -1, False))
    west = lax.ppermute(stack[:, :, -w:], "gx", shift_pairs(nx, 1, True))
    east = lax.ppermute(stack[:, :, :w], "gx", shift_pairs(nx, -1, True))
    south_west = lax.ppermute(stack[:, -w:, -w:], both, diag(1, 1))
    south_east = lax.ppermute(stack[:, -w:, :w], both, diag(1, -1))
    north_west = lax.ppermute(stack[:, :w, -w:], both, diag(-1, 1))
    north_east = lax.ppermute(stack[:, :w, :w], both, diag(-1, -1))
    folded = fold_strip(stack[:, -w:, :], fold_start, fold_rest, w) * signs
    at_top = lax.axis_index("gy") == ny - 1
    cols = stack.shape[-1]
    north = jnp.where(at_top, folded[:, :, w : w + cols], north)
    north_west = jnp.where(at_top, folded[:, :, :w], north_west)
    north_east = jnp.where(at_top, folded[:, :, w + cols :], north_east)
    return jnp.concatenate(
        [
            jnp.concatenate([south_west, south, south_east], axis=2),
            jnp.concatenate([west, stack, east], axis=2),
            jnp.concatenate([north_west, north, north_east], axis=2),
        ],
        axis=1,
    )


def crop(x, n):
    if n == 0:
        return x
    return x[..., n : x.shape[-2] - n, n : x.shape[-1] - n]


def compute_strain_rates(u_pad, v_pad):
    strain_rate_east = (u_pad[1:-1, 2:] - u_pad[1:-1, :-2]) * 0.5
    strain_rate_north = (v_pad[2:, 1:-1] - v_pad[:-2, 1:-1]) * 0.5
    strain_rate_shear = (
        u_pad[2:, 1:-1] - u_pad[:-2, 1:-1] + (v_pad[1:-1, 2:] - v_pad[1:-1, :-2])
    ) * 0.25
    return (strain_rate_east, strain_rate_north, strain_rate_shear)


def stress_update(old, strain_rate_east, strain_rate_north, strain_rate_shear, strength):
    divergence = strain_rate_east + strain_rate_north
    tension = strain_rate_east - strain_rate_north
    shear = 2.0 * strain_rate_shear
    delta = jnp.sqrt(divergence * divergence + (tension * tension + shear * shear) / ECC2 + DMIN2)
    zeta = strength / delta
    first = (old[0] + RELAX * (zeta * divergence - strength)) / (1.0 + RELAX)
    second = (old[1] + RELAX * zeta * tension / ECC2) / (1.0 + RELAX)
    third = (old[2] + RELAX * zeta * shear / (2.0 * ECC2)) / (1.0 + RELAX)
    return jnp.stack([first, second, third])


def stress_force(padded):
    normal_x = (padded[0] + padded[1]) * 0.5
    normal_y = (padded[0] - padded[1]) * 0.5
    shear = padded[2]
    eastward_force = (normal_x[1:-1, 2:] - normal_x[1:-1, :-2]) * 0.5 + (
        shear[2:, 1:-1] - shear[:-2, 1:-1]
    ) * 0.5
    northward_force = (shear[1:-1, 2:] - shear[1:-1, :-2]) * 0.5 + (
        normal_y[2:, 1:-1] - normal_y[:-2, 1:-1]
    ) * 0.5
    return (eastward_force, northward_force)


def momentum_solve(
    velocity,
    eastward_force,
    northward_force,
    wind,
    ocean_current_east,
    ocean_current_north,
    ice_mass_per_area,
    coriolis_parameter,
    velocity_mask,
):
    east = velocity[0]
    north = velocity[1]
    implicit_denominator = ice_mass_per_area + DTE * DRAG
    right_side_east = east * ice_mass_per_area + DTE * (
        eastward_force
        + wind[0]
        + DRAG * ocean_current_east
        + ice_mass_per_area * coriolis_parameter * north
    )
    right_side_north = north * ice_mass_per_area + DTE * (
        northward_force
        + wind[1]
        + DRAG * ocean_current_north
        - ice_mass_per_area * coriolis_parameter * east
    )
    return jnp.stack(
        [
            velocity_mask * right_side_east / implicit_denominator,
            velocity_mask * right_side_north / implicit_denominator,
        ]
    )


def column_growth(
    thickness,
    velocity,
    ocean_temp,
    ocean_salt,
    ocean_current_east,
    ocean_current_north,
    air_temp,
    omask,
):
    freeze = -0.054 * (SREF + ocean_salt)
    rel_east = velocity[0] - ocean_current_east
    rel_north = velocity[1] - ocean_current_north
    speed = jnp.sqrt(rel_east * rel_east + rel_north * rel_north + 0.01)
    melt = GAMMA * (ocean_temp - freeze) * speed
    growth = KAPPA * (freeze - air_temp) / (thickness + 0.1)
    return omask * jnp.maximum(thickness + DTT * (growth - melt), 0.0)


def body(
    ocean_blocks,
    block_map,
    velocity,
    stress,
    thickness,
    area,
    wind,
    air_temp,
    ice_presence_mask,
    ocean_land_mask,
    fold_partner_column,
):
    ocean = regroup_local(ocean_blocks, block_map)
    ocean_temp = ocean[:, 0, :]
    ocean_salt = ocean[:, 1, :]
    ocean_current_east = ocean[:, 2, :]
    ocean_current_north = ocean[:, 3, :]
    hsum = jnp.sum(area * thickness, axis=0)
    conc = jnp.sum(area, axis=0)
    strength = PSTAR * hsum * jnp.exp(-CSTAR * (1.0 - conc))
    ice_mass_per_area = hsum + 0.2
    rows = velocity.shape[1]
    cols = velocity.shape[2]
    total_rows = rows * lax.axis_size("gy")
    velocity_mask = (ice_presence_mask * ocean_land_mask).astype(jnp.float32)
    omask = ocean_land_mask.astype(jnp.float32)
    fold_col = fold_partner_column[0] % (cols * lax.axis_size("gx"))
    fold_start = fold_col // cols
    fold_rest = fold_col % cols

    width = 2 * ITERS
    stack = jnp.concatenate(
        [
            velocity,
            stress,
            strength[None],
            ice_mass_per_area[None],
            wind,
            ocean_current_east[None],
            ocean_current_north[None],
            velocity_mask[None],
        ],
        axis=0,
    )
    signs = jnp.array(
        [-1.0, -1.0, 1.0, 1.0, 1.0, 1.0, 1.0, -1.0, -1.0, -1.0, -1.0, 1.0], jnp.float32
    ).reshape(-1, 1, 1)
    ext = exchange(stack, width, signs, fold_start, fold_rest)
    grid_row = lax.axis_index("gy") * rows + jnp.arange(-width, rows + width, dtype=jnp.int32)
    true_row = jnp.where(grid_row > total_rows - 1, 2 * total_rows - 1 - grid_row, grid_row)
    coriolis_ext = (FCOR * (true_row.astype(jnp.float32) + 0.5) / float(total_rows))[:, None]
    inside_ext = (grid_row >= 0)[:, None]

    def rows_crop(x, n):
        return x if n == 0 else x[n : x.shape[0] - n]

    vel = ext[0:2]
    st = ext[2:5]
    st_radius = width
    for step in range(ITERS):
        radius = width - 2 * step
        e11, e22, e12 = compute_strain_rates(vel[0], vel[1])
        st = stress_update(
            crop(st, st_radius - (radius - 1)),
            e11,
            e22,
            e12,
            crop(ext[5], width - (radius - 1)),
        )
        st = jnp.where(rows_crop(inside_ext, width - (radius - 1)), st, 0.0)
        st_radius = radius - 1
        eastward_force, northward_force = stress_force(st)
        n = width - (radius - 2)
        vel = momentum_solve(
            crop(vel, 2),
            eastward_force,
            northward_force,
            crop(ext[7:9], n),
            crop(ext[9], n),
            crop(ext[10], n),
            crop(ext[6], n),
            rows_crop(coriolis_ext, n),
            crop(ext[11], n),
        )
        vel = jnp.where(rows_crop(inside_ext, n), vel, 0.0)
    velocity = vel
    stress = crop(st, st_radius)
    thickness_out = column_growth(
        thickness,
        velocity,
        ocean_temp,
        ocean_salt,
        ocean_current_east,
        ocean_current_north,
        air_temp,
        omask,
    )
    return (velocity, stress, thickness_out)


def solution(mesh):
    placed = (
        P("gy", None, "gx"),
        P("gy", "gx"),
        P(None, "gy", "gx"),
        P(None, "gy", "gx"),
        P(None, "gy", "gx"),
        P(None, "gy", "gx"),
        P(None, "gy", "gx"),
        P("gy", "gx"),
        P("gy", "gx"),
        P("gy", "gx"),
        P(),
    )
    return jax.shard_map(
        body,
        mesh=mesh,
        in_specs=placed,
        out_specs=(P(None, "gy", "gx"), P(None, "gy", "gx"), P(None, "gy", "gx")),
        check_vma=False,
    )
```

```python
import jax
import jax.numpy as jnp
from jax import lax
from jax.sharding import PartitionSpec as P

ITERS = 4


RELAX = 0.5
ECC2 = 4.0
DMIN2 = 0.01
PSTAR = 1.0
CSTAR = 5.0
DTE = 0.3
DRAG = 1.0
FCOR = 0.5
KAPPA = 0.5
GAMMA = 0.3
DTT = 0.5
SREF = 34.0


def shift_pairs(count, step, cyclic):
    pairs = [(i, i + step) for i in range(count) if 0 <= i + step < count]
    if cyclic:
        pairs = [(i, (i + step) % count) for i in range(count)]
    return pairs


def regroup_local(ocean_blocks, block_map):
    rows, fields, cols = ocean_blocks.shape
    peers = lax.axis_size("gx")
    group = max(2, rows // peers)
    count = rows // group
    target = block_map[:, 0]
    dest_dev = target[::group] // rows
    dest_row = (target % rows).reshape(count, group)
    chosen = dest_dev[None, :] == jnp.arange(peers, dtype=jnp.int32)[:, None]
    blocks = ocean_blocks.reshape(count, group * fields * cols)
    outgoing = jnp.dot(
        chosen.astype(jnp.float32),
        blocks,
        precision=lax.Precision.HIGHEST,
        preferred_element_type=jnp.float32,
    )
    labels = jnp.sum(jnp.where(chosen[:, :, None], dest_row[None, :, :] + 1, 0), axis=1) - 1
    packed = jnp.concatenate([outgoing, labels.astype(jnp.float32)], axis=1)
    arrived = lax.all_to_all(packed, "gx", split_axis=0, concat_axis=0, tiled=True)
    flat = arrived[:, : group * fields * cols].reshape(peers * group, fields * cols)
    arrived_rows = arrived[:, group * fields * cols :].astype(jnp.int32)
    picks = (
        arrived_rows.reshape(-1)[None, :] == jnp.arange(rows, dtype=jnp.int32)[:, None]
    ).astype(jnp.float32)
    local = jnp.dot(
        picks, flat, precision=lax.Precision.HIGHEST, preferred_element_type=jnp.float32
    )
    return local.reshape(rows, fields, cols)


def exchange(stack, width, signs, fold_start, fold_rest):
    ny = lax.axis_size("gy")
    nx = lax.axis_size("gx")
    w = width
    cols = stack.shape[-1]
    low = 8 if nx % 8 == 0 else 1
    a = fold_start // low
    b = fold_start % low

    def stage_one(aa):
        def run(top, west_in, east_in):
            mirrored = lax.ppermute(top, "gx", [(e, (low * aa - e) % nx) for e in range(nx)])
            west = lax.ppermute(west_in, "gx", shift_pairs(nx, 1, True))
            east = lax.ppermute(east_in, "gx", shift_pairs(nx, -1, True))
            return mirrored, west, east

        return run

    mirrored, west, east = lax.switch(
        a,
        [stage_one(aa) for aa in range(nx // low)],
        stack[:, -w:, :],
        stack[:, :, -w:],
        stack[:, :, :w],
    )
    wide = jnp.concatenate([west, stack, east], axis=2)

    def stage_two(bb):
        def run(y, south_in, north_in):
            parts = tuple(
                lax.ppermute(y, "gx", [(e, (e + bb + t) % nx) for e in range(nx)])
                for t in (-2, -1, 0, 1)
            )
            south = lax.ppermute(south_in, "gy", shift_pairs(ny, 1, False))
            north = lax.ppermute(north_in, "gy", shift_pairs(ny, -1, False))
            return parts, south, north

        return run

    parts, south, north = lax.switch(
        b, [stage_two(bb) for bb in range(low)], mirrored, wide[:, -w:, :], wide[:, :w, :]
    )
    strip = jnp.concatenate(parts, axis=-1)
    first = 2 * cols + fold_rest - (cols - 1) - w
    window = lax.dynamic_slice_in_dim(strip, first, cols + 2 * w, axis=2)
    folded = jnp.flip(window, axis=(1, 2)) * signs
    north = jnp.where(lax.axis_index("gy") == ny - 1, folded, north)
    return jnp.concatenate([south, wide, north], axis=1)


def crop(x, n):
    if n == 0:
        return x
    return x[..., n : x.shape[-2] - n, n : x.shape[-1] - n]


def compute_strain_rates(u_pad, v_pad):
    strain_rate_east = (u_pad[1:-1, 2:] - u_pad[1:-1, :-2]) * 0.5
    strain_rate_north = (v_pad[2:, 1:-1] - v_pad[:-2, 1:-1]) * 0.5
    strain_rate_shear = (
        u_pad[2:, 1:-1] - u_pad[:-2, 1:-1] + (v_pad[1:-1, 2:] - v_pad[1:-1, :-2])
    ) * 0.25
    return (strain_rate_east, strain_rate_north, strain_rate_shear)


def stress_update(old, strain_rate_east, strain_rate_north, strain_rate_shear, strength):
    divergence = strain_rate_east + strain_rate_north
    tension = strain_rate_east - strain_rate_north
    shear = 2.0 * strain_rate_shear
    delta = jnp.sqrt(divergence * divergence + (tension * tension + shear * shear) / ECC2 + DMIN2)
    zeta = strength / delta
    first = (old[0] + RELAX * (zeta * divergence - strength)) / (1.0 + RELAX)
    second = (old[1] + RELAX * zeta * tension / ECC2) / (1.0 + RELAX)
    third = (old[2] + RELAX * zeta * shear / (2.0 * ECC2)) / (1.0 + RELAX)
    return jnp.stack([first, second, third])


def stress_force(padded):
    normal_x = (padded[0] + padded[1]) * 0.5
    normal_y = (padded[0] - padded[1]) * 0.5
    shear = padded[2]
    eastward_force = (normal_x[1:-1, 2:] - normal_x[1:-1, :-2]) * 0.5 + (
        shear[2:, 1:-1] - shear[:-2, 1:-1]
    ) * 0.5
    northward_force = (shear[1:-1, 2:] - shear[1:-1, :-2]) * 0.5 + (
        normal_y[2:, 1:-1] - normal_y[:-2, 1:-1]
    ) * 0.5
    return (eastward_force, northward_force)


def momentum_solve(
    velocity,
    eastward_force,
    northward_force,
    wind,
    ocean_current_east,
    ocean_current_north,
    ice_mass_per_area,
    coriolis_parameter,
    velocity_mask,
):
    east = velocity[0]
    north = velocity[1]
    implicit_denominator = ice_mass_per_area + DTE * DRAG
    right_side_east = east * ice_mass_per_area + DTE * (
        eastward_force
        + wind[0]
        + DRAG * ocean_current_east
        + ice_mass_per_area * coriolis_parameter * north
    )
    right_side_north = north * ice_mass_per_area + DTE * (
        northward_force
        + wind[1]
        + DRAG * ocean_current_north
        - ice_mass_per_area * coriolis_parameter * east
    )
    return jnp.stack(
        [
            velocity_mask * right_side_east / implicit_denominator,
            velocity_mask * right_side_north / implicit_denominator,
        ]
    )


def column_growth(
    thickness,
    velocity,
    ocean_temp,
    ocean_salt,
    ocean_current_east,
    ocean_current_north,
    air_temp,
    omask,
):
    freeze = -0.054 * (SREF + ocean_salt)
    rel_east = velocity[0] - ocean_current_east
    rel_north = velocity[1] - ocean_current_north
    speed = jnp.sqrt(rel_east * rel_east + rel_north * rel_north + 0.01)
    melt = GAMMA * (ocean_temp - freeze) * speed
    growth = KAPPA * (freeze - air_temp) / (thickness + 0.1)
    return omask * jnp.maximum(thickness + DTT * (growth - melt), 0.0)


def body(
    ocean_blocks,
    block_map,
    velocity,
    stress,
    thickness,
    area,
    wind,
    air_temp,
    ice_presence_mask,
    ocean_land_mask,
    fold_partner_column,
):
    ocean = regroup_local(ocean_blocks, block_map)
    ocean_temp = ocean[:, 0, :]
    ocean_salt = ocean[:, 1, :]
    ocean_current_east = ocean[:, 2, :]
    ocean_current_north = ocean[:, 3, :]
    hsum = jnp.sum(area * thickness, axis=0)
    conc = jnp.sum(area, axis=0)
    strength = PSTAR * hsum * jnp.exp(-CSTAR * (1.0 - conc))
    ice_mass_per_area = hsum + 0.2
    rows = velocity.shape[1]
    cols = velocity.shape[2]
    total_rows = rows * lax.axis_size("gy")
    velocity_mask = (ice_presence_mask * ocean_land_mask).astype(jnp.float32)
    omask = ocean_land_mask.astype(jnp.float32)
    fold_col = fold_partner_column[0] % (cols * lax.axis_size("gx"))
    fold_start = fold_col // cols
    fold_rest = fold_col % cols

    width = 2 * ITERS
    stack = jnp.concatenate(
        [
            velocity,
            stress,
            strength[None],
            ice_mass_per_area[None],
            wind,
            ocean_current_east[None],
            ocean_current_north[None],
            velocity_mask[None],
        ],
        axis=0,
    )
    signs = jnp.array(
        [-1.0, -1.0, 1.0, 1.0, 1.0, 1.0, 1.0, -1.0, -1.0, -1.0, -1.0, 1.0], jnp.float32
    ).reshape(-1, 1, 1)
    ext = exchange(stack, width, signs, fold_start, fold_rest)
    grid_row = lax.axis_index("gy") * rows + jnp.arange(-width, rows + width, dtype=jnp.int32)
    true_row = jnp.where(grid_row > total_rows - 1, 2 * total_rows - 1 - grid_row, grid_row)
    coriolis_ext = (FCOR * (true_row.astype(jnp.float32) + 0.5) / float(total_rows))[:, None]
    inside_ext = (grid_row >= 0)[:, None]

    def rows_crop(x, n):
        return x if n == 0 else x[n : x.shape[0] - n]

    vel = ext[0:2]
    st = ext[2:5]
    st_radius = width
    for step in range(ITERS):
        radius = width - 2 * step
        e11, e22, e12 = compute_strain_rates(vel[0], vel[1])
        st = stress_update(
            crop(st, st_radius - (radius - 1)),
            e11,
            e22,
            e12,
            crop(ext[5], width - (radius - 1)),
        )
        st = jnp.where(rows_crop(inside_ext, width - (radius - 1)), st, 0.0)
        st_radius = radius - 1
        eastward_force, northward_force = stress_force(st)
        n = width - (radius - 2)
        vel = momentum_solve(
            crop(vel, 2),
            eastward_force,
            northward_force,
            crop(ext[7:9], n),
            crop(ext[9], n),
            crop(ext[10], n),
            crop(ext[6], n),
            rows_crop(coriolis_ext, n),
            crop(ext[11], n),
        )
        vel = jnp.where(rows_crop(inside_ext, n), vel, 0.0)
    velocity = vel
    stress = crop(st, st_radius)
    thickness_out = column_growth(
        thickness,
        velocity,
        ocean_temp,
        ocean_salt,
        ocean_current_east,
        ocean_current_north,
        air_temp,
        omask,
    )
    return (velocity, stress, thickness_out)


def solution(mesh):
    placed = (
        P("gy", None, "gx"),
        P("gy", "gx"),
        P(None, "gy", "gx"),
        P(None, "gy", "gx"),
        P(None, "gy", "gx"),
        P(None, "gy", "gx"),
        P(None, "gy", "gx"),
        P("gy", "gx"),
        P("gy", "gx"),
        P("gy", "gx"),
        P(),
    )
    return jax.shard_map(
        body,
        mesh=mesh,
        in_specs=placed,
        out_specs=(P(None, "gy", "gx"), P(None, "gy", "gx"), P(None, "gy", "gx")),
        check_vma=False,
    )
```

```python
import jax
import jax.numpy as jnp
from jax import lax
from jax.sharding import PartitionSpec as P

ITERS = 4


RELAX = 0.5
ECC2 = 4.0
DMIN2 = 0.01
PSTAR = 1.0
CSTAR = 5.0
DTE = 0.3
DRAG = 1.0
FCOR = 0.5
KAPPA = 0.5
GAMMA = 0.3
DTT = 0.5
SREF = 34.0


def shift_pairs(count, step, cyclic):
    pairs = [(i, i + step) for i in range(count) if 0 <= i + step < count]
    if cyclic:
        pairs = [(i, (i + step) % count) for i in range(count)]
    return pairs


def regroup_local(ocean_blocks, block_map):
    rows, fields, cols = ocean_blocks.shape
    peers = lax.axis_size("gx")
    group = max(2, rows // peers)
    count = rows // group
    target = block_map[:, 0]
    dest_dev = target[::group] // rows
    dest_row = (target % rows).reshape(count, group)
    chosen = dest_dev[None, :] == jnp.arange(peers, dtype=jnp.int32)[:, None]
    blocks = ocean_blocks.reshape(count, group * fields * cols)
    outgoing = jnp.dot(
        chosen.astype(jnp.float32),
        blocks,
        precision=lax.Precision.HIGHEST,
        preferred_element_type=jnp.float32,
    )
    labels = jnp.sum(jnp.where(chosen[:, :, None], dest_row[None, :, :] + 1, 0), axis=1) - 1
    packed = jnp.concatenate([outgoing, labels.astype(jnp.float32)], axis=1)
    arrived = lax.all_to_all(packed, "gx", split_axis=0, concat_axis=0, tiled=True)
    flat = arrived[:, : group * fields * cols].reshape(peers * group, fields * cols)
    arrived_rows = arrived[:, group * fields * cols :].astype(jnp.int32)
    picks = (
        arrived_rows.reshape(-1)[None, :] == jnp.arange(rows, dtype=jnp.int32)[:, None]
    ).astype(jnp.float32)
    local = jnp.dot(
        picks, flat, precision=lax.Precision.HIGHEST, preferred_element_type=jnp.float32
    )
    return local.reshape(rows, fields, cols)


def exchange(stack, width, signs, fold_start, fold_rest):
    ny = lax.axis_size("gy")
    nx = lax.axis_size("gx")
    w = width
    cols = stack.shape[-1]
    low = 8 if nx % 8 == 0 else 1
    a = fold_start // low
    b = fold_start % low
    top_row = (ny - 1) * nx
    both = ("gy", "gx")

    def on_top(target):
        return [(top_row + e, top_row + target(e) % nx) for e in range(nx)]

    def stage_one(aa):
        def run(top, west_in, east_in):
            mirrored = lax.ppermute(top, both, on_top(lambda e: low * aa - e))
            west = lax.ppermute(west_in, "gx", shift_pairs(nx, 1, True))
            east = lax.ppermute(east_in, "gx", shift_pairs(nx, -1, True))
            return mirrored, west, east

        return run

    mirrored, west, east = lax.switch(
        a,
        [stage_one(aa) for aa in range(nx // low)],
        stack[:, -w:, :],
        stack[:, :, -w:],
        stack[:, :, :w],
    )
    wide = jnp.concatenate([west, stack, east], axis=2)
    spans = ((-2, -1, 0), (-1, 0, 1))
    span = jnp.where(fold_rest < w - 1, 0, 1)

    def stage_two(bb, ts):
        def run(y, south_in, north_in):
            parts = [
                lax.ppermute(y, both, on_top(lambda e, t=t: e + bb + t)) for t in ts
            ]
            south = lax.ppermute(south_in, "gy", shift_pairs(ny, 1, False))
            north = lax.ppermute(north_in, "gy", shift_pairs(ny, -1, False))
            return tuple(parts), south, north

        return run

    parts, south, north = lax.switch(
        b * len(spans) + span,
        [stage_two(bb, ts) for bb in range(low) for ts in spans],
        mirrored,
        wide[:, -w:, :],
        wide[:, :w, :],
    )
    strip = jnp.concatenate(parts, axis=-1)
    lowest = jnp.where(span == 0, 2, 1)
    first = lowest * cols + fold_rest - (cols - 1) - w
    window = lax.dynamic_slice_in_dim(strip, first, cols + 2 * w, axis=2)
    folded = jnp.flip(window, axis=(1, 2)) * signs
    north = jnp.where(lax.axis_index("gy") == ny - 1, folded, north)
    return jnp.concatenate([south, wide, north], axis=1)


def crop(x, n):
    if n == 0:
        return x
    return x[..., n : x.shape[-2] - n, n : x.shape[-1] - n]


def compute_strain_rates(u_pad, v_pad):
    strain_rate_east = (u_pad[1:-1, 2:] - u_pad[1:-1, :-2]) * 0.5
    strain_rate_north = (v_pad[2:, 1:-1] - v_pad[:-2, 1:-1]) * 0.5
    strain_rate_shear = (
        u_pad[2:, 1:-1] - u_pad[:-2, 1:-1] + (v_pad[1:-1, 2:] - v_pad[1:-1, :-2])
    ) * 0.25
    return (strain_rate_east, strain_rate_north, strain_rate_shear)


def stress_update(old, strain_rate_east, strain_rate_north, strain_rate_shear, strength):
    divergence = strain_rate_east + strain_rate_north
    tension = strain_rate_east - strain_rate_north
    shear = 2.0 * strain_rate_shear
    delta = jnp.sqrt(divergence * divergence + (tension * tension + shear * shear) / ECC2 + DMIN2)
    zeta = strength / delta
    first = (old[0] + RELAX * (zeta * divergence - strength)) / (1.0 + RELAX)
    second = (old[1] + RELAX * zeta * tension / ECC2) / (1.0 + RELAX)
    third = (old[2] + RELAX * zeta * shear / (2.0 * ECC2)) / (1.0 + RELAX)
    return jnp.stack([first, second, third])


def stress_force(padded):
    normal_x = (padded[0] + padded[1]) * 0.5
    normal_y = (padded[0] - padded[1]) * 0.5
    shear = padded[2]
    eastward_force = (normal_x[1:-1, 2:] - normal_x[1:-1, :-2]) * 0.5 + (
        shear[2:, 1:-1] - shear[:-2, 1:-1]
    ) * 0.5
    northward_force = (shear[1:-1, 2:] - shear[1:-1, :-2]) * 0.5 + (
        normal_y[2:, 1:-1] - normal_y[:-2, 1:-1]
    ) * 0.5
    return (eastward_force, northward_force)


def momentum_solve(
    velocity,
    eastward_force,
    northward_force,
    forcing,
    ice_mass_per_area,
    coriolis_parameter,
    velocity_mask,
):
    east = velocity[0]
    north = velocity[1]
    implicit_denominator = ice_mass_per_area + DTE * DRAG
    right_side_east = east * ice_mass_per_area + DTE * (
        eastward_force + forcing[0] + ice_mass_per_area * coriolis_parameter * north
    )
    right_side_north = north * ice_mass_per_area + DTE * (
        northward_force + forcing[1] - ice_mass_per_area * coriolis_parameter * east
    )
    return jnp.stack(
        [
            velocity_mask * right_side_east / implicit_denominator,
            velocity_mask * right_side_north / implicit_denominator,
        ]
    )


def column_growth(
    thickness,
    velocity,
    ocean_temp,
    ocean_salt,
    ocean_current_east,
    ocean_current_north,
    air_temp,
    omask,
):
    freeze = -0.054 * (SREF + ocean_salt)
    rel_east = velocity[0] - ocean_current_east
    rel_north = velocity[1] - ocean_current_north
    speed = jnp.sqrt(rel_east * rel_east + rel_north * rel_north + 0.01)
    melt = GAMMA * (ocean_temp - freeze) * speed
    growth = KAPPA * (freeze - air_temp) / (thickness + 0.1)
    return omask * jnp.maximum(thickness + DTT * (growth - melt), 0.0)


def body(
    ocean_blocks,
    block_map,
    velocity,
    stress,
    thickness,
    area,
    wind,
    air_temp,
    ice_presence_mask,
    ocean_land_mask,
    fold_partner_column,
):
    ocean = regroup_local(ocean_blocks, block_map)
    ocean_temp = ocean[:, 0, :]
    ocean_salt = ocean[:, 1, :]
    ocean_current_east = ocean[:, 2, :]
    ocean_current_north = ocean[:, 3, :]
    hsum = jnp.sum(area * thickness, axis=0)
    conc = jnp.sum(area, axis=0)
    strength = PSTAR * hsum * jnp.exp(-CSTAR * (1.0 - conc))
    ice_mass_per_area = hsum + 0.2
    rows = velocity.shape[1]
    cols = velocity.shape[2]
    total_rows = rows * lax.axis_size("gy")
    velocity_mask = (ice_presence_mask * ocean_land_mask).astype(jnp.float32)
    omask = ocean_land_mask.astype(jnp.float32)
    fold_col = fold_partner_column[0] % (cols * lax.axis_size("gx"))
    fold_start = fold_col // cols
    fold_rest = fold_col % cols

    width = 2 * ITERS
    stack = jnp.concatenate(
        [
            velocity,
            stress,
            strength[None],
            ice_mass_per_area[None],
            wind + DRAG * jnp.stack([ocean_current_east, ocean_current_north]),
            velocity_mask[None],
        ],
        axis=0,
    )
    signs = jnp.array(
        [-1.0, -1.0, 1.0, 1.0, 1.0, 1.0, 1.0, -1.0, -1.0, 1.0], jnp.float32
    ).reshape(-1, 1, 1)
    ext = exchange(stack, width, signs, fold_start, fold_rest)
    grid_row = lax.axis_index("gy") * rows + jnp.arange(-width, rows + width, dtype=jnp.int32)
    true_row = jnp.where(grid_row > total_rows - 1, 2 * total_rows - 1 - grid_row, grid_row)
    coriolis_ext = (FCOR * (true_row.astype(jnp.float32) + 0.5) / float(total_rows))[:, None]
    inside_ext = (grid_row >= 0)[:, None]

    def rows_crop(x, n):
        return x if n == 0 else x[n : x.shape[0] - n]

    vel = ext[0:2]
    st = ext[2:5]
    st_radius = width
    for step in range(ITERS):
        radius = width - 2 * step
        e11, e22, e12 = compute_strain_rates(vel[0], vel[1])
        st = stress_update(
            crop(st, st_radius - (radius - 1)),
            e11,
            e22,
            e12,
            crop(ext[5], width - (radius - 1)),
        )
        st = jnp.where(rows_crop(inside_ext, width - (radius - 1)), st, 0.0)
        st_radius = radius - 1
        eastward_force, northward_force = stress_force(st)
        n = width - (radius - 2)
        vel = momentum_solve(
            crop(vel, 2),
            eastward_force,
            northward_force,
            crop(ext[7:9], n),
            crop(ext[6], n),
            rows_crop(coriolis_ext, n),
            crop(ext[9], n),
        )
        vel = jnp.where(rows_crop(inside_ext, n), vel, 0.0)
    velocity = vel
    stress = crop(st, st_radius)
    thickness_out = column_growth(
        thickness,
        velocity,
        ocean_temp,
        ocean_salt,
        ocean_current_east,
        ocean_current_north,
        air_temp,
        omask,
    )
    return (velocity, stress, thickness_out)


def solution(mesh):
    placed = (
        P("gy", None, "gx"),
        P("gy", "gx"),
        P(None, "gy", "gx"),
        P(None, "gy", "gx"),
        P(None, "gy", "gx"),
        P(None, "gy", "gx"),
        P(None, "gy", "gx"),
        P("gy", "gx"),
        P("gy", "gx"),
        P("gy", "gx"),
        P(),
    )
    return jax.shard_map(
        body,
        mesh=mesh,
        in_specs=placed,
        out_specs=(P(None, "gy", "gx"), P(None, "gy", "gx"), P(None, "gy", "gx")),
        check_vma=False,
    )
```

```python
import jax
import jax.numpy as jnp
from jax import lax
from jax.sharding import PartitionSpec as P

ITERS = 4


RELAX = 0.5
ECC2 = 4.0
DMIN2 = 0.01
PSTAR = 1.0
CSTAR = 5.0
DTE = 0.3
DRAG = 1.0
FCOR = 0.5
KAPPA = 0.5
GAMMA = 0.3
DTT = 0.5
SREF = 34.0


def shift_pairs(count, step, cyclic):
    pairs = [(i, i + step) for i in range(count) if 0 <= i + step < count]
    if cyclic:
        pairs = [(i, (i + step) % count) for i in range(count)]
    return pairs


def regroup_local(ocean_blocks, block_map):
    rows, fields, cols = ocean_blocks.shape
    peers = lax.axis_size("gx")
    group = max(2, rows // peers)
    count = rows // group
    target = block_map[:, 0]
    dest_dev = target[::group] // rows
    dest_row = (target % rows).reshape(count, group)
    chosen = dest_dev[None, :] == jnp.arange(peers, dtype=jnp.int32)[:, None]
    blocks = ocean_blocks.reshape(count, group * fields * cols)
    outgoing = jnp.dot(
        chosen.astype(jnp.float32),
        blocks,
        precision=lax.Precision.HIGHEST,
        preferred_element_type=jnp.float32,
    )
    labels = jnp.sum(jnp.where(chosen[:, :, None], dest_row[None, :, :] + 1, 0), axis=1) - 1
    packed = jnp.concatenate([outgoing, labels.astype(jnp.float32)], axis=1)
    arrived = lax.all_to_all(packed, "gx", split_axis=0, concat_axis=0, tiled=True)
    flat = arrived[:, : group * fields * cols].reshape(peers * group, fields * cols)
    arrived_rows = arrived[:, group * fields * cols :].astype(jnp.int32)
    picks = (
        arrived_rows.reshape(-1)[None, :] == jnp.arange(rows, dtype=jnp.int32)[:, None]
    ).astype(jnp.float32)
    local = jnp.dot(
        picks, flat, precision=lax.Precision.HIGHEST, preferred_element_type=jnp.float32
    )
    return local.reshape(rows, fields, cols)


def exchange(stack, width, signs, fold_start, fold_rest):
    ny = lax.axis_size("gy")
    nx = lax.axis_size("gx")
    w = width
    cols = stack.shape[-1]
    low = 8 if nx % 8 == 0 else 1
    a = fold_start // low
    b = fold_start % low
    top_row = (ny - 1) * nx
    both = ("gy", "gx")

    def on_top(target):
        return [(top_row + e, top_row + target(e) % nx) for e in range(nx)]

    def stage_one(aa):
        def run(top, west_in, east_in):
            mirrored = lax.ppermute(top, both, on_top(lambda e: low * aa - e))
            west = lax.ppermute(west_in, "gx", shift_pairs(nx, 1, True))
            east = lax.ppermute(east_in, "gx", shift_pairs(nx, -1, True))
            return mirrored, west, east

        return run

    mirrored, west, east = lax.switch(
        a,
        [stage_one(aa) for aa in range(nx // low)],
        stack[:, -w:, :],
        stack[:, :, -w:],
        stack[:, :, :w],
    )
    wide = jnp.concatenate([west, stack, east], axis=2)
    spans = ((-2, -1, 0), (-1, 0, 1))
    span = jnp.where(fold_rest < w - 1, 0, 1)

    def stage_two(bb, ts):
        def run(y, south_in, north_in):
            parts = [
                lax.ppermute(y, both, on_top(lambda e, t=t: e + bb + t)) for t in ts
            ]
            south = lax.ppermute(south_in, "gy", shift_pairs(ny, 1, False))
            north = lax.ppermute(north_in, "gy", shift_pairs(ny, -1, False))
            return tuple(parts), south, north

        return run

    parts, south, north = lax.switch(
        b * len(spans) + span,
        [stage_two(bb, ts) for bb in range(low) for ts in spans],
        mirrored,
        wide[:, -w:, :],
        wide[:, :w, :],
    )
    strip = jnp.concatenate(parts, axis=-1)
    lowest = jnp.where(span == 0, 2, 1)
    first = lowest * cols + fold_rest - (cols - 1) - w
    window = lax.dynamic_slice_in_dim(strip, first, cols + 2 * w, axis=2)
    folded = jnp.flip(window, axis=(1, 2)) * signs
    north = jnp.where(lax.axis_index("gy") == ny - 1, folded, north)
    return jnp.concatenate([south, wide, north], axis=1)


def crop(x, n):
    if n == 0:
        return x
    return x[..., n : x.shape[-2] - n, n : x.shape[-1] - n]


def compute_strain_rates(u_pad, v_pad):
    strain_rate_east = (u_pad[1:-1, 2:] - u_pad[1:-1, :-2]) * 0.5
    strain_rate_north = (v_pad[2:, 1:-1] - v_pad[:-2, 1:-1]) * 0.5
    strain_rate_shear = (
        u_pad[2:, 1:-1] - u_pad[:-2, 1:-1] + (v_pad[1:-1, 2:] - v_pad[1:-1, :-2])
    ) * 0.25
    return (strain_rate_east, strain_rate_north, strain_rate_shear)


def stress_update(old, strain_rate_east, strain_rate_north, strain_rate_shear, strength):
    divergence = strain_rate_east + strain_rate_north
    tension = strain_rate_east - strain_rate_north
    shear = 2.0 * strain_rate_shear
    delta = jnp.sqrt(divergence * divergence + (tension * tension + shear * shear) / ECC2 + DMIN2)
    zeta = strength / delta
    first = (old[0] + RELAX * (zeta * divergence - strength)) / (1.0 + RELAX)
    second = (old[1] + RELAX * zeta * tension / ECC2) / (1.0 + RELAX)
    third = (old[2] + RELAX * zeta * shear / (2.0 * ECC2)) / (1.0 + RELAX)
    return jnp.stack([first, second, third])


def stress_force(padded):
    normal_x = (padded[0] + padded[1]) * 0.5
    normal_y = (padded[0] - padded[1]) * 0.5
    shear = padded[2]
    eastward_force = (normal_x[1:-1, 2:] - normal_x[1:-1, :-2]) * 0.5 + (
        shear[2:, 1:-1] - shear[:-2, 1:-1]
    ) * 0.5
    northward_force = (shear[1:-1, 2:] - shear[1:-1, :-2]) * 0.5 + (
        normal_y[2:, 1:-1] - normal_y[:-2, 1:-1]
    ) * 0.5
    return (eastward_force, northward_force)


def momentum_solve(
    velocity,
    eastward_force,
    northward_force,
    forcing,
    ice_mass_per_area,
    coriolis_parameter,
    velocity_mask,
):
    east = velocity[0]
    north = velocity[1]
    implicit_denominator = ice_mass_per_area + DTE * DRAG
    right_side_east = east * ice_mass_per_area + DTE * (
        eastward_force + forcing[0] + ice_mass_per_area * coriolis_parameter * north
    )
    right_side_north = north * ice_mass_per_area + DTE * (
        northward_force + forcing[1] - ice_mass_per_area * coriolis_parameter * east
    )
    return jnp.stack(
        [
            velocity_mask * right_side_east / implicit_denominator,
            velocity_mask * right_side_north / implicit_denominator,
        ]
    )


def column_growth(
    thickness,
    velocity,
    ocean_temp,
    ocean_salt,
    ocean_current_east,
    ocean_current_north,
    air_temp,
    omask,
):
    freeze = -0.054 * (SREF + ocean_salt)
    rel_east = velocity[0] - ocean_current_east
    rel_north = velocity[1] - ocean_current_north
    speed = jnp.sqrt(rel_east * rel_east + rel_north * rel_north + 0.01)
    melt = GAMMA * (ocean_temp - freeze) * speed
    growth = KAPPA * (freeze - air_temp) / (thickness + 0.1)
    return omask * jnp.maximum(thickness + DTT * (growth - melt), 0.0)


def body(
    ocean_blocks,
    block_map,
    velocity,
    stress,
    thickness,
    area,
    wind,
    air_temp,
    ice_presence_mask,
    ocean_land_mask,
    fold_partner_column,
):
    hsum = jnp.sum(area * thickness, axis=0)
    conc = jnp.sum(area, axis=0)
    strength = PSTAR * hsum * jnp.exp(-CSTAR * (1.0 - conc))
    ice_mass_per_area = hsum + 0.2
    rows = velocity.shape[1]
    cols = velocity.shape[2]
    total_rows = rows * lax.axis_size("gy")
    velocity_mask = (ice_presence_mask * ocean_land_mask).astype(jnp.float32)
    omask = ocean_land_mask.astype(jnp.float32)
    fold_col = fold_partner_column[0] % (cols * lax.axis_size("gx"))
    fold_start = fold_col // cols
    fold_rest = fold_col % cols

    width = 2 * ITERS
    stack = jnp.concatenate(
        [
            velocity,
            stress,
            strength[None],
            ice_mass_per_area[None],
            wind,
            velocity_mask[None],
        ],
        axis=0,
    )
    signs = jnp.array(
        [-1.0, -1.0, 1.0, 1.0, 1.0, 1.0, 1.0, -1.0, -1.0, 1.0], jnp.float32
    ).reshape(-1, 1, 1)
    ext_early = exchange(stack, width, signs, fold_start, fold_rest)
    ocean = regroup_local(ocean_blocks, block_map)
    ocean_temp = ocean[:, 0, :]
    ocean_salt = ocean[:, 1, :]
    ocean_current_east = ocean[:, 2, :]
    ocean_current_north = ocean[:, 3, :]
    current_ext = exchange(
        jnp.stack([ocean_current_east, ocean_current_north]),
        width,
        -jnp.ones((2, 1, 1), jnp.float32),
        fold_start,
        fold_rest,
    )
    ext = jnp.concatenate(
        [
            ext_early[:7],
            ext_early[7:9] + DRAG * current_ext,
            ext_early[9:10],
        ],
        axis=0,
    )
    grid_row = lax.axis_index("gy") * rows + jnp.arange(-width, rows + width, dtype=jnp.int32)
    true_row = jnp.where(grid_row > total_rows - 1, 2 * total_rows - 1 - grid_row, grid_row)
    coriolis_ext = (FCOR * (true_row.astype(jnp.float32) + 0.5) / float(total_rows))[:, None]
    inside_ext = (grid_row >= 0)[:, None]

    def rows_crop(x, n):
        return x if n == 0 else x[n : x.shape[0] - n]

    vel = ext[0:2]
    st = ext[2:5]
    st_radius = width
    for step in range(ITERS):
        radius = width - 2 * step
        e11, e22, e12 = compute_strain_rates(vel[0], vel[1])
        st = stress_update(
            crop(st, st_radius - (radius - 1)),
            e11,
            e22,
            e12,
            crop(ext[5], width - (radius - 1)),
        )
        st = jnp.where(rows_crop(inside_ext, width - (radius - 1)), st, 0.0)
        st_radius = radius - 1
        eastward_force, northward_force = stress_force(st)
        n = width - (radius - 2)
        vel = momentum_solve(
            crop(vel, 2),
            eastward_force,
            northward_force,
            crop(ext[7:9], n),
            crop(ext[6], n),
            rows_crop(coriolis_ext, n),
            crop(ext[9], n),
        )
        vel = jnp.where(rows_crop(inside_ext, n), vel, 0.0)
    velocity = vel
    stress = crop(st, st_radius)
    thickness_out = column_growth(
        thickness,
        velocity,
        ocean_temp,
        ocean_salt,
        ocean_current_east,
        ocean_current_north,
        air_temp,
        omask,
    )
    return (velocity, stress, thickness_out)


def solution(mesh):
    placed = (
        P("gy", None, "gx"),
        P("gy", "gx"),
        P(None, "gy", "gx"),
        P(None, "gy", "gx"),
        P(None, "gy", "gx"),
        P(None, "gy", "gx"),
        P(None, "gy", "gx"),
        P("gy", "gx"),
        P("gy", "gx"),
        P("gy", "gx"),
        P(),
    )
    return jax.shard_map(
        body,
        mesh=mesh,
        in_specs=placed,
        out_specs=(P(None, "gy", "gx"), P(None, "gy", "gx"), P(None, "gy", "gx")),
        check_vma=False,
    )
```

```python
import jax
import jax.numpy as jnp
from jax import lax
from jax.sharding import PartitionSpec as P

ITERS = 4


RELAX = 0.5
ECC2 = 4.0
DMIN2 = 0.01
PSTAR = 1.0
CSTAR = 5.0
DTE = 0.3
DRAG = 1.0
FCOR = 0.5
KAPPA = 0.5
GAMMA = 0.3
DTT = 0.5
SREF = 34.0


def shift_pairs(count, step, cyclic):
    pairs = [(i, i + step) for i in range(count) if 0 <= i + step < count]
    if cyclic:
        pairs = [(i, (i + step) % count) for i in range(count)]
    return pairs


def regroup_local(ocean_blocks, block_map):
    rows, fields, cols = ocean_blocks.shape
    peers = lax.axis_size("gx")
    group = max(2, rows // peers)
    count = rows // group
    target = block_map[:, 0]
    dest_dev = target[::group] // rows
    dest_row = (target % rows).reshape(count, group)
    chosen = dest_dev[None, :] == jnp.arange(peers, dtype=jnp.int32)[:, None]
    blocks = ocean_blocks.reshape(count, group * fields * cols)
    outgoing = jnp.dot(
        chosen.astype(jnp.float32),
        blocks,
        precision=lax.Precision.HIGHEST,
        preferred_element_type=jnp.float32,
    )
    labels = jnp.sum(jnp.where(chosen[:, :, None], dest_row[None, :, :] + 1, 0), axis=1) - 1
    packed = jnp.concatenate([outgoing, labels.astype(jnp.float32)], axis=1)
    arrived = lax.all_to_all(packed, "gx", split_axis=0, concat_axis=0, tiled=True)
    flat = arrived[:, : group * fields * cols].reshape(peers * group, fields * cols)
    arrived_rows = arrived[:, group * fields * cols :].astype(jnp.int32)
    picks = (
        arrived_rows.reshape(-1)[None, :] == jnp.arange(rows, dtype=jnp.int32)[:, None]
    ).astype(jnp.float32)
    local = jnp.dot(
        picks, flat, precision=lax.Precision.HIGHEST, preferred_element_type=jnp.float32
    )
    return local.reshape(rows, fields, cols)


def exchange(stack, width, signs, fold_start, fold_rest):
    ny = lax.axis_size("gy")
    nx = lax.axis_size("gx")
    w = width
    cols = stack.shape[-1]
    low = 4 if nx % 4 == 0 else 1
    a = fold_start // low
    b = fold_start % low
    top_row = (ny - 1) * nx
    both = ("gy", "gx")

    def on_top(target):
        return [(top_row + e, top_row + target(e) % nx) for e in range(nx)]

    def stage_one(aa):
        def run(top, west_in, east_in):
            mirrored = lax.ppermute(top, both, on_top(lambda e: low * aa - e))
            west = lax.ppermute(west_in, "gx", shift_pairs(nx, 1, True))
            east = lax.ppermute(east_in, "gx", shift_pairs(nx, -1, True))
            return mirrored, west, east

        return run

    mirrored, west, east = lax.switch(
        a,
        [stage_one(aa) for aa in range(nx // low)],
        stack[:, -w:, :],
        stack[:, :, -w:],
        stack[:, :, :w],
    )
    wide = jnp.concatenate([west, stack, east], axis=2)
    spans = ((-2, -1, 0), (-1, 0, 1))
    span = jnp.where(fold_rest < w - 1, 0, 1)

    def stage_two(bb, ts):
        def run(y, south_in, north_in):
            parts = [
                lax.ppermute(y, both, on_top(lambda e, t=t: e + bb + t)) for t in ts
            ]
            south = lax.ppermute(south_in, "gy", shift_pairs(ny, 1, False))
            north = lax.ppermute(north_in, "gy", shift_pairs(ny, -1, False))
            return tuple(parts), south, north

        return run

    parts, south, north = lax.switch(
        b * len(spans) + span,
        [stage_two(bb, ts) for bb in range(low) for ts in spans],
        mirrored,
        wide[:, -w:, :],
        wide[:, :w, :],
    )
    strip = jnp.concatenate(parts, axis=-1)
    lowest = jnp.where(span == 0, 2, 1)
    first = lowest * cols + fold_rest - (cols - 1) - w
    window = lax.dynamic_slice_in_dim(strip, first, cols + 2 * w, axis=2)
    folded = jnp.flip(window, axis=(1, 2)) * signs
    north = jnp.where(lax.axis_index("gy") == ny - 1, folded, north)
    return jnp.concatenate([south, wide, north], axis=1)


def crop(x, n):
    if n == 0:
        return x
    return x[..., n : x.shape[-2] - n, n : x.shape[-1] - n]


def compute_strain_rates(u_pad, v_pad):
    strain_rate_east = (u_pad[1:-1, 2:] - u_pad[1:-1, :-2]) * 0.5
    strain_rate_north = (v_pad[2:, 1:-1] - v_pad[:-2, 1:-1]) * 0.5
    strain_rate_shear = (
        u_pad[2:, 1:-1] - u_pad[:-2, 1:-1] + (v_pad[1:-1, 2:] - v_pad[1:-1, :-2])
    ) * 0.25
    return (strain_rate_east, strain_rate_north, strain_rate_shear)


def stress_update(old, strain_rate_east, strain_rate_north, strain_rate_shear, strength):
    divergence = strain_rate_east + strain_rate_north
    tension = strain_rate_east - strain_rate_north
    shear = 2.0 * strain_rate_shear
    delta = jnp.sqrt(divergence * divergence + (tension * tension + shear * shear) / ECC2 + DMIN2)
    zeta = strength / delta
    first = (old[0] + RELAX * (zeta * divergence - strength)) / (1.0 + RELAX)
    second = (old[1] + RELAX * zeta * tension / ECC2) / (1.0 + RELAX)
    third = (old[2] + RELAX * zeta * shear / (2.0 * ECC2)) / (1.0 + RELAX)
    return jnp.stack([first, second, third])


def stress_force(padded):
    normal_x = (padded[0] + padded[1]) * 0.5
    normal_y = (padded[0] - padded[1]) * 0.5
    shear = padded[2]
    eastward_force = (normal_x[1:-1, 2:] - normal_x[1:-1, :-2]) * 0.5 + (
        shear[2:, 1:-1] - shear[:-2, 1:-1]
    ) * 0.5
    northward_force = (shear[1:-1, 2:] - shear[1:-1, :-2]) * 0.5 + (
        normal_y[2:, 1:-1] - normal_y[:-2, 1:-1]
    ) * 0.5
    return (eastward_force, northward_force)


def momentum_solve(
    velocity,
    eastward_force,
    northward_force,
    forcing,
    ice_mass_per_area,
    coriolis_parameter,
    velocity_mask,
):
    east = velocity[0]
    north = velocity[1]
    implicit_denominator = ice_mass_per_area + DTE * DRAG
    right_side_east = east * ice_mass_per_area + DTE * (
        eastward_force + forcing[0] + ice_mass_per_area * coriolis_parameter * north
    )
    right_side_north = north * ice_mass_per_area + DTE * (
        northward_force + forcing[1] - ice_mass_per_area * coriolis_parameter * east
    )
    return jnp.stack(
        [
            velocity_mask * right_side_east / implicit_denominator,
            velocity_mask * right_side_north / implicit_denominator,
        ]
    )


def column_growth(
    thickness,
    velocity,
    ocean_temp,
    ocean_salt,
    ocean_current_east,
    ocean_current_north,
    air_temp,
    omask,
):
    freeze = -0.054 * (SREF + ocean_salt)
    rel_east = velocity[0] - ocean_current_east
    rel_north = velocity[1] - ocean_current_north
    speed = jnp.sqrt(rel_east * rel_east + rel_north * rel_north + 0.01)
    melt = GAMMA * (ocean_temp - freeze) * speed
    growth = KAPPA * (freeze - air_temp) / (thickness + 0.1)
    return omask * jnp.maximum(thickness + DTT * (growth - melt), 0.0)


def body(
    ocean_blocks,
    block_map,
    velocity,
    stress,
    thickness,
    area,
    wind,
    air_temp,
    ice_presence_mask,
    ocean_land_mask,
    fold_partner_column,
):
    ocean = regroup_local(ocean_blocks, block_map)
    ocean_temp = ocean[:, 0, :]
    ocean_salt = ocean[:, 1, :]
    ocean_current_east = ocean[:, 2, :]
    ocean_current_north = ocean[:, 3, :]
    hsum = jnp.sum(area * thickness, axis=0)
    conc = jnp.sum(area, axis=0)
    strength = PSTAR * hsum * jnp.exp(-CSTAR * (1.0 - conc))
    ice_mass_per_area = hsum + 0.2
    rows = velocity.shape[1]
    cols = velocity.shape[2]
    total_rows = rows * lax.axis_size("gy")
    velocity_mask = (ice_presence_mask * ocean_land_mask).astype(jnp.float32)
    omask = ocean_land_mask.astype(jnp.float32)
    fold_col = fold_partner_column[0] % (cols * lax.axis_size("gx"))
    fold_start = fold_col // cols
    fold_rest = fold_col % cols

    width = 2 * ITERS
    stack = jnp.concatenate(
        [
            velocity,
            stress,
            strength[None],
            ice_mass_per_area[None],
            wind + DRAG * jnp.stack([ocean_current_east, ocean_current_north]),
            velocity_mask[None],
        ],
        axis=0,
    )
    signs = jnp.array(
        [-1.0, -1.0, 1.0, 1.0, 1.0, 1.0, 1.0, -1.0, -1.0, 1.0], jnp.float32
    ).reshape(-1, 1, 1)
    ext = exchange(stack, width, signs, fold_start, fold_rest)
    grid_row = lax.axis_index("gy") * rows + jnp.arange(-width, rows + width, dtype=jnp.int32)
    true_row = jnp.where(grid_row > total_rows - 1, 2 * total_rows - 1 - grid_row, grid_row)
    coriolis_ext = (FCOR * (true_row.astype(jnp.float32) + 0.5) / float(total_rows))[:, None]
    inside_ext = (grid_row >= 0)[:, None]

    def rows_crop(x, n):
        return x if n == 0 else x[n : x.shape[0] - n]

    vel = ext[0:2]
    st = ext[2:5]
    st_radius = width
    for step in range(ITERS):
        radius = width - 2 * step
        e11, e22, e12 = compute_strain_rates(vel[0], vel[1])
        st = stress_update(
            crop(st, st_radius - (radius - 1)),
            e11,
            e22,
            e12,
            crop(ext[5], width - (radius - 1)),
        )
        st = jnp.where(rows_crop(inside_ext, width - (radius - 1)), st, 0.0)
        st_radius = radius - 1
        eastward_force, northward_force = stress_force(st)
        n = width - (radius - 2)
        vel = momentum_solve(
            crop(vel, 2),
            eastward_force,
            northward_force,
            crop(ext[7:9], n),
            crop(ext[6], n),
            rows_crop(coriolis_ext, n),
            crop(ext[9], n),
        )
        vel = jnp.where(rows_crop(inside_ext, n), vel, 0.0)
    velocity = vel
    stress = crop(st, st_radius)
    thickness_out = column_growth(
        thickness,
        velocity,
        ocean_temp,
        ocean_salt,
        ocean_current_east,
        ocean_current_north,
        air_temp,
        omask,
    )
    return (velocity, stress, thickness_out)


def solution(mesh):
    placed = (
        P("gy", None, "gx"),
        P("gy", "gx"),
        P(None, "gy", "gx"),
        P(None, "gy", "gx"),
        P(None, "gy", "gx"),
        P(None, "gy", "gx"),
        P(None, "gy", "gx"),
        P("gy", "gx"),
        P("gy", "gx"),
        P("gy", "gx"),
        P(),
    )
    return jax.shard_map(
        body,
        mesh=mesh,
        in_specs=placed,
        out_specs=(P(None, "gy", "gx"), P(None, "gy", "gx"), P(None, "gy", "gx")),
        check_vma=False,
    )
```

```python
import jax
import jax.numpy as jnp
from jax import lax
from jax.sharding import PartitionSpec as P

ITERS = 4


RELAX = 0.5
ECC2 = 4.0
DMIN2 = 0.01
PSTAR = 1.0
CSTAR = 5.0
DTE = 0.3
DRAG = 1.0
FCOR = 0.5
KAPPA = 0.5
GAMMA = 0.3
DTT = 0.5
SREF = 34.0


def shift_pairs(count, step, cyclic):
    pairs = [(i, i + step) for i in range(count) if 0 <= i + step < count]
    if cyclic:
        pairs = [(i, (i + step) % count) for i in range(count)]
    return pairs


def regroup_local(ocean_blocks, block_map):
    rows, fields, cols = ocean_blocks.shape
    peers = lax.axis_size("gx")
    group = max(2, rows // peers)
    count = rows // group
    target = block_map[:, 0]
    dest_dev = target[::group] // rows
    dest_row = (target % rows).reshape(count, group)
    chosen = dest_dev[None, :] == jnp.arange(peers, dtype=jnp.int32)[:, None]
    blocks = ocean_blocks.reshape(count, group * fields * cols)
    outgoing = jnp.dot(
        chosen.astype(jnp.float32),
        blocks,
        precision=lax.Precision.HIGHEST,
        preferred_element_type=jnp.float32,
    )
    labels = jnp.sum(jnp.where(chosen[:, :, None], dest_row[None, :, :] + 1, 0), axis=1) - 1
    packed = jnp.concatenate([outgoing, labels.astype(jnp.float32)], axis=1)
    arrived = lax.all_to_all(packed, "gx", split_axis=0, concat_axis=0, tiled=True)
    flat = arrived[:, : group * fields * cols].reshape(peers * group, fields * cols)
    arrived_rows = arrived[:, group * fields * cols :].astype(jnp.int32)
    picks = (
        arrived_rows.reshape(-1)[None, :] == jnp.arange(rows, dtype=jnp.int32)[:, None]
    ).astype(jnp.float32)
    local = jnp.dot(
        picks, flat, precision=lax.Precision.HIGHEST, preferred_element_type=jnp.float32
    )
    return local.reshape(rows, fields, cols)


def exchange(stack, width, signs, fold_start, fold_rest):
    ny = lax.axis_size("gy")
    nx = lax.axis_size("gx")
    w = width
    cols = stack.shape[-1]
    low = 4 if nx % 4 == 0 else 1
    a = fold_start // low
    b = fold_start % low
    top_row = (ny - 1) * nx
    both = ("gy", "gx")

    def on_top(target):
        return [(top_row + e, top_row + target(e) % nx) for e in range(nx)]

    def stage_one(aa):
        def run(top, west_in, east_in):
            mirrored = lax.ppermute(top, both, on_top(lambda e: low * aa - e))
            west = lax.ppermute(west_in, "gx", shift_pairs(nx, 1, True))
            east = lax.ppermute(east_in, "gx", shift_pairs(nx, -1, True))
            return mirrored, west, east

        return run

    mirrored, west, east = lax.switch(
        a,
        [stage_one(aa) for aa in range(nx // low)],
        stack[:, -w:, :],
        stack[:, :, -w:],
        stack[:, :, :w],
    )
    wide = jnp.concatenate([west, stack, east], axis=2)
    spans = ((-2, -1, 0), (-1, 0), (-1, 0, 1))
    span = jnp.where(fold_rest < w - 1, 0, jnp.where(fold_rest > cols - 1 - w, 2, 1))

    def stage_two(bb, ts):
        def run(y, south_in, north_in):
            parts = [
                lax.ppermute(y, both, on_top(lambda e, t=t: e + bb + t)) for t in ts
            ]
            parts += [jnp.zeros_like(y)] * (3 - len(ts))
            south = lax.ppermute(south_in, "gy", shift_pairs(ny, 1, False))
            north = lax.ppermute(north_in, "gy", shift_pairs(ny, -1, False))
            return tuple(parts), south, north

        return run

    parts, south, north = lax.switch(
        b * len(spans) + span,
        [stage_two(bb, ts) for bb in range(low) for ts in spans],
        mirrored,
        wide[:, -w:, :],
        wide[:, :w, :],
    )
    strip = jnp.concatenate(parts, axis=-1)
    lowest = jnp.where(span == 0, 2, 1)
    first = lowest * cols + fold_rest - (cols - 1) - w
    window = lax.dynamic_slice_in_dim(strip, first, cols + 2 * w, axis=2)
    folded = jnp.flip(window, axis=(1, 2)) * signs
    north = jnp.where(lax.axis_index("gy") == ny - 1, folded, north)
    return jnp.concatenate([south, wide, north], axis=1)


def crop(x, n):
    if n == 0:
        return x
    return x[..., n : x.shape[-2] - n, n : x.shape[-1] - n]


def compute_strain_rates(u_pad, v_pad):
    strain_rate_east = (u_pad[1:-1, 2:] - u_pad[1:-1, :-2]) * 0.5
    strain_rate_north = (v_pad[2:, 1:-1] - v_pad[:-2, 1:-1]) * 0.5
    strain_rate_shear = (
        u_pad[2:, 1:-1] - u_pad[:-2, 1:-1] + (v_pad[1:-1, 2:] - v_pad[1:-1, :-2])
    ) * 0.25
    return (strain_rate_east, strain_rate_north, strain_rate_shear)


def stress_update(old, strain_rate_east, strain_rate_north, strain_rate_shear, strength):
    divergence = strain_rate_east + strain_rate_north
    tension = strain_rate_east - strain_rate_north
    shear = 2.0 * strain_rate_shear
    delta = jnp.sqrt(divergence * divergence + (tension * tension + shear * shear) / ECC2 + DMIN2)
    zeta = strength / delta
    first = (old[0] + RELAX * (zeta * divergence - strength)) / (1.0 + RELAX)
    second = (old[1] + RELAX * zeta * tension / ECC2) / (1.0 + RELAX)
    third = (old[2] + RELAX * zeta * shear / (2.0 * ECC2)) / (1.0 + RELAX)
    return jnp.stack([first, second, third])


def stress_force(padded):
    normal_x = (padded[0] + padded[1]) * 0.5
    normal_y = (padded[0] - padded[1]) * 0.5
    shear = padded[2]
    eastward_force = (normal_x[1:-1, 2:] - normal_x[1:-1, :-2]) * 0.5 + (
        shear[2:, 1:-1] - shear[:-2, 1:-1]
    ) * 0.5
    northward_force = (shear[1:-1, 2:] - shear[1:-1, :-2]) * 0.5 + (
        normal_y[2:, 1:-1] - normal_y[:-2, 1:-1]
    ) * 0.5
    return (eastward_force, northward_force)


def momentum_solve(
    velocity,
    eastward_force,
    northward_force,
    forcing,
    ice_mass_per_area,
    coriolis_parameter,
    velocity_mask,
):
    east = velocity[0]
    north = velocity[1]
    implicit_denominator = ice_mass_per_area + DTE * DRAG
    right_side_east = east * ice_mass_per_area + DTE * (
        eastward_force + forcing[0] + ice_mass_per_area * coriolis_parameter * north
    )
    right_side_north = north * ice_mass_per_area + DTE * (
        northward_force + forcing[1] - ice_mass_per_area * coriolis_parameter * east
    )
    return jnp.stack(
        [
            velocity_mask * right_side_east / implicit_denominator,
            velocity_mask * right_side_north / implicit_denominator,
        ]
    )


def column_growth(
    thickness,
    velocity,
    ocean_temp,
    ocean_salt,
    ocean_current_east,
    ocean_current_north,
    air_temp,
    omask,
):
    freeze = -0.054 * (SREF + ocean_salt)
    rel_east = velocity[0] - ocean_current_east
    rel_north = velocity[1] - ocean_current_north
    speed = jnp.sqrt(rel_east * rel_east + rel_north * rel_north + 0.01)
    melt = GAMMA * (ocean_temp - freeze) * speed
    growth = KAPPA * (freeze - air_temp) / (thickness + 0.1)
    return omask * jnp.maximum(thickness + DTT * (growth - melt), 0.0)


def body(
    ocean_blocks,
    block_map,
    velocity,
    stress,
    thickness,
    area,
    wind,
    air_temp,
    ice_presence_mask,
    ocean_land_mask,
    fold_partner_column,
):
    ocean = regroup_local(ocean_blocks, block_map)
    ocean_temp = ocean[:, 0, :]
    ocean_salt = ocean[:, 1, :]
    ocean_current_east = ocean[:, 2, :]
    ocean_current_north = ocean[:, 3, :]
    hsum = jnp.sum(area * thickness, axis=0)
    conc = jnp.sum(area, axis=0)
    strength = PSTAR * hsum * jnp.exp(-CSTAR * (1.0 - conc))
    ice_mass_per_area = hsum + 0.2
    rows = velocity.shape[1]
    cols = velocity.shape[2]
    total_rows = rows * lax.axis_size("gy")
    velocity_mask = (ice_presence_mask * ocean_land_mask).astype(jnp.float32)
    omask = ocean_land_mask.astype(jnp.float32)
    fold_col = fold_partner_column[0] % (cols * lax.axis_size("gx"))
    fold_start = fold_col // cols
    fold_rest = fold_col % cols

    width = 2 * ITERS
    stack = jnp.concatenate(
        [
            velocity,
            stress,
            strength[None],
            ice_mass_per_area[None],
            wind + DRAG * jnp.stack([ocean_current_east, ocean_current_north]),
            velocity_mask[None],
        ],
        axis=0,
    )
    signs = jnp.array(
        [-1.0, -1.0, 1.0, 1.0, 1.0, 1.0, 1.0, -1.0, -1.0, 1.0], jnp.float32
    ).reshape(-1, 1, 1)
    ext = exchange(stack, width, signs, fold_start, fold_rest)
    grid_row = lax.axis_index("gy") * rows + jnp.arange(-width, rows + width, dtype=jnp.int32)
    true_row = jnp.where(grid_row > total_rows - 1, 2 * total_rows - 1 - grid_row, grid_row)
    coriolis_ext = (FCOR * (true_row.astype(jnp.float32) + 0.5) / float(total_rows))[:, None]
    inside_ext = (grid_row >= 0)[:, None]

    def rows_crop(x, n):
        return x if n == 0 else x[n : x.shape[0] - n]

    vel = ext[0:2]
    st = ext[2:5]
    st_radius = width
    for step in range(ITERS):
        radius = width - 2 * step
        e11, e22, e12 = compute_strain_rates(vel[0], vel[1])
        st = stress_update(
            crop(st, st_radius - (radius - 1)),
            e11,
            e22,
            e12,
            crop(ext[5], width - (radius - 1)),
        )
        st = jnp.where(rows_crop(inside_ext, width - (radius - 1)), st, 0.0)
        st_radius = radius - 1
        eastward_force, northward_force = stress_force(st)
        n = width - (radius - 2)
        vel = momentum_solve(
            crop(vel, 2),
            eastward_force,
            northward_force,
            crop(ext[7:9], n),
            crop(ext[6], n),
            rows_crop(coriolis_ext, n),
            crop(ext[9], n),
        )
        vel = jnp.where(rows_crop(inside_ext, n), vel, 0.0)
    velocity = vel
    stress = crop(st, st_radius)
    thickness_out = column_growth(
        thickness,
        velocity,
        ocean_temp,
        ocean_salt,
        ocean_current_east,
        ocean_current_north,
        air_temp,
        omask,
    )
    return (velocity, stress, thickness_out)


def solution(mesh):
    placed = (
        P("gy", None, "gx"),
        P("gy", "gx"),
        P(None, "gy", "gx"),
        P(None, "gy", "gx"),
        P(None, "gy", "gx"),
        P(None, "gy", "gx"),
        P(None, "gy", "gx"),
        P("gy", "gx"),
        P("gy", "gx"),
        P("gy", "gx"),
        P(),
    )
    return jax.shard_map(
        body,
        mesh=mesh,
        in_specs=placed,
        out_specs=(P(None, "gy", "gx"), P(None, "gy", "gx"), P(None, "gy", "gx")),
        check_vma=False,
    )
```

```python
import jax
import jax.numpy as jnp
from jax import lax
from jax.sharding import PartitionSpec as P

ITERS = 4


RELAX = 0.5
ECC2 = 4.0
DMIN2 = 0.01
PSTAR = 1.0
CSTAR = 5.0
DTE = 0.3
DRAG = 1.0
FCOR = 0.5
KAPPA = 0.5
GAMMA = 0.3
DTT = 0.5
SREF = 34.0


def shift_pairs(count, step, cyclic):
    pairs = [(i, i + step) for i in range(count) if 0 <= i + step < count]
    if cyclic:
        pairs = [(i, (i + step) % count) for i in range(count)]
    return pairs


def regroup_local(ocean_blocks, block_map, width):
    rows, fields, cols = ocean_blocks.shape
    peers = lax.axis_size("gx")
    group = max(2, rows // peers)
    count = rows // group
    target = block_map[:, 0]
    dest_dev = target[::group] // rows
    dest_row = (target % rows).reshape(count, group)
    devices = jnp.arange(peers, dtype=jnp.int32)
    blocks = ocean_blocks.reshape(count, group, fields, cols)
    currents = blocks[:, :, 2:4, :]

    def pack(dest, payload):
        chosen = dest[None, :] == devices[:, None]
        out = jnp.dot(
            chosen.astype(jnp.float32),
            payload.reshape(count, -1),
            precision=lax.Precision.HIGHEST,
            preferred_element_type=jnp.float32,
        )
        labels = jnp.sum(jnp.where(chosen[:, :, None], dest_row[None, :, :] + 1, 0), axis=1) - 1
        return out, labels.astype(jnp.float32)

    main, main_rows = pack(dest_dev, blocks)
    west, west_rows = pack((dest_dev + 1) % peers, currents[..., cols - width :])
    east, east_rows = pack((dest_dev - 1) % peers, currents[..., :width])
    pieces = [main, west, east, main_rows, west_rows, east_rows]
    arrived = lax.all_to_all(
        jnp.concatenate(pieces, axis=1), "gx", split_axis=0, concat_axis=0, tiled=True
    )
    bounds = [0]
    for piece in pieces:
        bounds.append(bounds[-1] + piece.shape[1])
    part = [arrived[:, bounds[i] : bounds[i + 1]] for i in range(len(pieces))]

    def unpack(data, labels):
        flat = data.reshape(peers * group, -1)
        picks = (
            labels.astype(jnp.int32).reshape(-1)[None, :]
            == jnp.arange(rows, dtype=jnp.int32)[:, None]
        ).astype(jnp.float32)
        return jnp.dot(
            picks, flat, precision=lax.Precision.HIGHEST, preferred_element_type=jnp.float32
        )

    local = unpack(part[0], part[3]).reshape(rows, fields, cols)
    west_rim = unpack(part[1], part[4]).reshape(rows, 2, width).transpose(1, 0, 2)
    east_rim = unpack(part[2], part[5]).reshape(rows, 2, width).transpose(1, 0, 2)
    return local, west_rim, east_rim


def exchange(stack, west, east, width, signs, fold_start, fold_rest):
    ny = lax.axis_size("gy")
    nx = lax.axis_size("gx")
    w = width
    cols = stack.shape[-1]
    low = 4 if nx % 4 == 0 else 1
    a = fold_start // low
    b = fold_start % low
    top_row = (ny - 1) * nx
    both = ("gy", "gx")

    def on_top(target):
        return [(top_row + e, top_row + target(e) % nx) for e in range(nx)]

    def stage_one(aa):
        return lambda top: lax.ppermute(top, both, on_top(lambda e: low * aa - e))

    mirrored = lax.switch(a, [stage_one(aa) for aa in range(nx // low)], stack[:, -w:, :])
    wide = jnp.concatenate([west, stack, east], axis=2)
    spans = ((-2, -1, 0), (-1, 0), (-1, 0, 1))
    span = jnp.where(fold_rest < w - 1, 0, jnp.where(fold_rest > cols - 1 - w, 2, 1))

    def stage_two(bb, ts):
        def run(y, south_in, north_in):
            parts = [
                lax.ppermute(y, both, on_top(lambda e, t=t: e + bb + t)) for t in ts
            ]
            parts += [jnp.zeros_like(y)] * (3 - len(ts))
            south = lax.ppermute(south_in, "gy", shift_pairs(ny, 1, False))
            north = lax.ppermute(north_in, "gy", shift_pairs(ny, -1, False))
            return tuple(parts), south, north

        return run

    parts, south, north = lax.switch(
        b * len(spans) + span,
        [stage_two(bb, ts) for bb in range(low) for ts in spans],
        mirrored,
        wide[:, -w:, :],
        wide[:, :w, :],
    )
    strip = jnp.concatenate(parts, axis=-1)
    lowest = jnp.where(span == 0, 2, 1)
    first = lowest * cols + fold_rest - (cols - 1) - w
    window = lax.dynamic_slice_in_dim(strip, first, cols + 2 * w, axis=2)
    folded = jnp.flip(window, axis=(1, 2)) * signs
    north = jnp.where(lax.axis_index("gy") == ny - 1, folded, north)
    return jnp.concatenate([south, wide, north], axis=1)


def crop(x, n):
    if n == 0:
        return x
    return x[..., n : x.shape[-2] - n, n : x.shape[-1] - n]


def compute_strain_rates(u_pad, v_pad):
    strain_rate_east = (u_pad[1:-1, 2:] - u_pad[1:-1, :-2]) * 0.5
    strain_rate_north = (v_pad[2:, 1:-1] - v_pad[:-2, 1:-1]) * 0.5
    strain_rate_shear = (
        u_pad[2:, 1:-1] - u_pad[:-2, 1:-1] + (v_pad[1:-1, 2:] - v_pad[1:-1, :-2])
    ) * 0.25
    return (strain_rate_east, strain_rate_north, strain_rate_shear)


def stress_update(old, strain_rate_east, strain_rate_north, strain_rate_shear, strength):
    divergence = strain_rate_east + strain_rate_north
    tension = strain_rate_east - strain_rate_north
    shear = 2.0 * strain_rate_shear
    delta = jnp.sqrt(divergence * divergence + (tension * tension + shear * shear) / ECC2 + DMIN2)
    zeta = strength / delta
    first = (old[0] + RELAX * (zeta * divergence - strength)) / (1.0 + RELAX)
    second = (old[1] + RELAX * zeta * tension / ECC2) / (1.0 + RELAX)
    third = (old[2] + RELAX * zeta * shear / (2.0 * ECC2)) / (1.0 + RELAX)
    return jnp.stack([first, second, third])


def stress_force(padded):
    normal_x = (padded[0] + padded[1]) * 0.5
    normal_y = (padded[0] - padded[1]) * 0.5
    shear = padded[2]
    eastward_force = (normal_x[1:-1, 2:] - normal_x[1:-1, :-2]) * 0.5 + (
        shear[2:, 1:-1] - shear[:-2, 1:-1]
    ) * 0.5
    northward_force = (shear[1:-1, 2:] - shear[1:-1, :-2]) * 0.5 + (
        normal_y[2:, 1:-1] - normal_y[:-2, 1:-1]
    ) * 0.5
    return (eastward_force, northward_force)


def momentum_solve(
    velocity,
    eastward_force,
    northward_force,
    forcing,
    ice_mass_per_area,
    coriolis_parameter,
    velocity_mask,
):
    east = velocity[0]
    north = velocity[1]
    implicit_denominator = ice_mass_per_area + DTE * DRAG
    right_side_east = east * ice_mass_per_area + DTE * (
        eastward_force + forcing[0] + ice_mass_per_area * coriolis_parameter * north
    )
    right_side_north = north * ice_mass_per_area + DTE * (
        northward_force + forcing[1] - ice_mass_per_area * coriolis_parameter * east
    )
    return jnp.stack(
        [
            velocity_mask * right_side_east / implicit_denominator,
            velocity_mask * right_side_north / implicit_denominator,
        ]
    )


def column_growth(
    thickness,
    velocity,
    ocean_temp,
    ocean_salt,
    ocean_current_east,
    ocean_current_north,
    air_temp,
    omask,
):
    freeze = -0.054 * (SREF + ocean_salt)
    rel_east = velocity[0] - ocean_current_east
    rel_north = velocity[1] - ocean_current_north
    speed = jnp.sqrt(rel_east * rel_east + rel_north * rel_north + 0.01)
    melt = GAMMA * (ocean_temp - freeze) * speed
    growth = KAPPA * (freeze - air_temp) / (thickness + 0.1)
    return omask * jnp.maximum(thickness + DTT * (growth - melt), 0.0)


def body(
    ocean_blocks,
    block_map,
    velocity,
    stress,
    thickness,
    area,
    wind,
    air_temp,
    ice_presence_mask,
    ocean_land_mask,
    fold_partner_column,
):
    hsum = jnp.sum(area * thickness, axis=0)
    conc = jnp.sum(area, axis=0)
    strength = PSTAR * hsum * jnp.exp(-CSTAR * (1.0 - conc))
    ice_mass_per_area = hsum + 0.2
    rows = velocity.shape[1]
    cols = velocity.shape[2]
    total_rows = rows * lax.axis_size("gy")
    velocity_mask = (ice_presence_mask * ocean_land_mask).astype(jnp.float32)
    omask = ocean_land_mask.astype(jnp.float32)
    fold_col = fold_partner_column[0] % (cols * lax.axis_size("gx"))
    fold_start = fold_col // cols
    fold_rest = fold_col % cols

    width = 2 * ITERS
    nx = lax.axis_size("gx")
    early = jnp.concatenate(
        [velocity, stress, strength[None], ice_mass_per_area[None], wind, velocity_mask[None]],
        axis=0,
    )
    west_early = lax.ppermute(early[:, :, -width:], "gx", shift_pairs(nx, 1, True))
    east_early = lax.ppermute(early[:, :, :width], "gx", shift_pairs(nx, -1, True))
    ocean, current_west, current_east = regroup_local(ocean_blocks, block_map, width)
    ocean_temp = ocean[:, 0, :]
    ocean_salt = ocean[:, 1, :]
    ocean_current_east = ocean[:, 2, :]
    ocean_current_north = ocean[:, 3, :]
    currents = jnp.stack([ocean_current_east, ocean_current_north])

    def with_forcing(fields, current):
        return jnp.concatenate(
            [fields[:7], fields[7:9] + DRAG * current, fields[9:10]], axis=0
        )

    stack = with_forcing(early, currents)
    signs = jnp.array(
        [-1.0, -1.0, 1.0, 1.0, 1.0, 1.0, 1.0, -1.0, -1.0, 1.0], jnp.float32
    ).reshape(-1, 1, 1)
    ext = exchange(
        stack,
        with_forcing(west_early, current_west),
        with_forcing(east_early, current_east),
        width,
        signs,
        fold_start,
        fold_rest,
    )
    grid_row = lax.axis_index("gy") * rows + jnp.arange(-width, rows + width, dtype=jnp.int32)
    true_row = jnp.where(grid_row > total_rows - 1, 2 * total_rows - 1 - grid_row, grid_row)
    coriolis_ext = (FCOR * (true_row.astype(jnp.float32) + 0.5) / float(total_rows))[:, None]
    inside_ext = (grid_row >= 0)[:, None]

    def rows_crop(x, n):
        return x if n == 0 else x[n : x.shape[0] - n]

    vel = ext[0:2]
    st = ext[2:5]
    st_radius = width
    for step in range(ITERS):
        radius = width - 2 * step
        e11, e22, e12 = compute_strain_rates(vel[0], vel[1])
        st = stress_update(
            crop(st, st_radius - (radius - 1)),
            e11,
            e22,
            e12,
            crop(ext[5], width - (radius - 1)),
        )
        st = jnp.where(rows_crop(inside_ext, width - (radius - 1)), st, 0.0)
        st_radius = radius - 1
        eastward_force, northward_force = stress_force(st)
        n = width - (radius - 2)
        vel = momentum_solve(
            crop(vel, 2),
            eastward_force,
            northward_force,
            crop(ext[7:9], n),
            crop(ext[6], n),
            rows_crop(coriolis_ext, n),
            crop(ext[9], n),
        )
        vel = jnp.where(rows_crop(inside_ext, n), vel, 0.0)
    velocity = vel
    stress = crop(st, st_radius)
    thickness_out = column_growth(
        thickness,
        velocity,
        ocean_temp,
        ocean_salt,
        ocean_current_east,
        ocean_current_north,
        air_temp,
        omask,
    )
    return (velocity, stress, thickness_out)


def solution(mesh):
    placed = (
        P("gy", None, "gx"),
        P("gy", "gx"),
        P(None, "gy", "gx"),
        P(None, "gy", "gx"),
        P(None, "gy", "gx"),
        P(None, "gy", "gx"),
        P(None, "gy", "gx"),
        P("gy", "gx"),
        P("gy", "gx"),
        P("gy", "gx"),
        P(),
    )
    return jax.shard_map(
        body,
        mesh=mesh,
        in_specs=placed,
        out_specs=(P(None, "gy", "gx"), P(None, "gy", "gx"), P(None, "gy", "gx")),
        check_vma=False,
    )
```

```python
import jax
import jax.numpy as jnp
from jax import lax
from jax.sharding import PartitionSpec as P

ITERS = 4


RELAX = 0.5
ECC2 = 4.0
DMIN2 = 0.01
PSTAR = 1.0
CSTAR = 5.0
DTE = 0.3
DRAG = 1.0
FCOR = 0.5
KAPPA = 0.5
GAMMA = 0.3
DTT = 0.5
SREF = 34.0


def shift_pairs(count, step, cyclic):
    pairs = [(i, i + step) for i in range(count) if 0 <= i + step < count]
    if cyclic:
        pairs = [(i, (i + step) % count) for i in range(count)]
    return pairs


def regroup_local(ocean_blocks, block_map):
    rows, fields, cols = ocean_blocks.shape
    peers = lax.axis_size("gx")
    group = max(2, rows // peers)
    count = rows // group
    target = block_map[:, 0]
    dest_dev = target[::group] // rows
    dest_row = (target % rows).reshape(count, group)
    chosen = dest_dev[None, :] == jnp.arange(peers, dtype=jnp.int32)[:, None]
    blocks = ocean_blocks.reshape(count, group * fields * cols)
    outgoing = jnp.dot(
        chosen.astype(jnp.float32),
        blocks,
        precision=lax.Precision.HIGHEST,
        preferred_element_type=jnp.float32,
    )
    labels = jnp.sum(jnp.where(chosen[:, :, None], dest_row[None, :, :] + 1, 0), axis=1) - 1
    packed = jnp.concatenate([outgoing, labels.astype(jnp.float32)], axis=1)
    arrived = lax.all_to_all(packed, "gx", split_axis=0, concat_axis=0, tiled=True)
    flat = arrived[:, : group * fields * cols].reshape(peers * group, fields * cols)
    arrived_rows = arrived[:, group * fields * cols :].astype(jnp.int32)
    picks = (
        arrived_rows.reshape(-1)[None, :] == jnp.arange(rows, dtype=jnp.int32)[:, None]
    ).astype(jnp.float32)
    local = jnp.dot(
        picks, flat, precision=lax.Precision.HIGHEST, preferred_element_type=jnp.float32
    )
    return local.reshape(rows, fields, cols)


def exchange(stack, width, signs, fold_start, fold_rest):
    ny = lax.axis_size("gy")
    nx = lax.axis_size("gx")
    w = width
    cols = stack.shape[-1]
    low = 4 if nx % 4 == 0 else 1
    a = fold_start // low
    b = fold_start % low
    top_row = (ny - 1) * nx
    both = ("gy", "gx")

    def on_top(target):
        return [(top_row + e, top_row + target(e) % nx) for e in range(nx)]

    def stage_one(aa):
        def run(top, west_in, east_in):
            mirrored = lax.ppermute(top, both, on_top(lambda e: low * aa - e))
            west = lax.ppermute(west_in, "gx", shift_pairs(nx, 1, True))
            east = lax.ppermute(east_in, "gx", shift_pairs(nx, -1, True))
            return mirrored, west, east

        return run

    mirrored, west, east = lax.switch(
        a,
        [stage_one(aa) for aa in range(nx // low)],
        stack[:, -w:, :],
        stack[:, :, -w:],
        stack[:, :, :w],
    )
    wide = jnp.concatenate([west, stack, east], axis=2)
    spans = ((-2, -1, 0), (-1, 0), (-1, 0, 1))
    span = jnp.where(fold_rest < w - 1, 0, jnp.where(fold_rest > cols - 1 - w, 2, 1))

    def stage_two(bb, ts):
        def run(y, south_in, north_in):
            south = lax.ppermute(south_in, "gy", shift_pairs(ny, 1, False))
            north = lax.ppermute(north_in, "gy", shift_pairs(ny, -1, False))
            parts = [
                lax.ppermute(y, both, on_top(lambda e, t=t: e + bb + t)) for t in ts
            ]
            parts += [jnp.zeros_like(y)] * (3 - len(ts))
            return tuple(parts), south, north

        return run

    parts, south, north = lax.switch(
        b * len(spans) + span,
        [stage_two(bb, ts) for bb in range(low) for ts in spans],
        mirrored,
        wide[:, -w:, :],
        wide[:, :w, :],
    )
    strip = jnp.concatenate(parts, axis=-1)
    lowest = jnp.where(span == 0, 2, 1)
    first = lowest * cols + fold_rest - (cols - 1) - w
    window = lax.dynamic_slice_in_dim(strip, first, cols + 2 * w, axis=2)
    folded = jnp.flip(window, axis=(1, 2)) * signs
    north = jnp.where(lax.axis_index("gy") == ny - 1, folded, north)
    return jnp.concatenate([south, wide, north], axis=1)


def crop(x, n):
    if n == 0:
        return x
    return x[..., n : x.shape[-2] - n, n : x.shape[-1] - n]


def compute_strain_rates(u_pad, v_pad):
    strain_rate_east = (u_pad[1:-1, 2:] - u_pad[1:-1, :-2]) * 0.5
    strain_rate_north = (v_pad[2:, 1:-1] - v_pad[:-2, 1:-1]) * 0.5
    strain_rate_shear = (
        u_pad[2:, 1:-1] - u_pad[:-2, 1:-1] + (v_pad[1:-1, 2:] - v_pad[1:-1, :-2])
    ) * 0.25
    return (strain_rate_east, strain_rate_north, strain_rate_shear)


def stress_update(old, strain_rate_east, strain_rate_north, strain_rate_shear, strength):
    divergence = strain_rate_east + strain_rate_north
    tension = strain_rate_east - strain_rate_north
    shear = 2.0 * strain_rate_shear
    delta = jnp.sqrt(divergence * divergence + (tension * tension + shear * shear) / ECC2 + DMIN2)
    zeta = strength / delta
    first = (old[0] + RELAX * (zeta * divergence - strength)) / (1.0 + RELAX)
    second = (old[1] + RELAX * zeta * tension / ECC2) / (1.0 + RELAX)
    third = (old[2] + RELAX * zeta * shear / (2.0 * ECC2)) / (1.0 + RELAX)
    return jnp.stack([first, second, third])


def stress_force(padded):
    normal_x = (padded[0] + padded[1]) * 0.5
    normal_y = (padded[0] - padded[1]) * 0.5
    shear = padded[2]
    eastward_force = (normal_x[1:-1, 2:] - normal_x[1:-1, :-2]) * 0.5 + (
        shear[2:, 1:-1] - shear[:-2, 1:-1]
    ) * 0.5
    northward_force = (shear[1:-1, 2:] - shear[1:-1, :-2]) * 0.5 + (
        normal_y[2:, 1:-1] - normal_y[:-2, 1:-1]
    ) * 0.5
    return (eastward_force, northward_force)


def momentum_solve(
    velocity,
    eastward_force,
    northward_force,
    forcing,
    ice_mass_per_area,
    coriolis_parameter,
    velocity_mask,
):
    east = velocity[0]
    north = velocity[1]
    implicit_denominator = ice_mass_per_area + DTE * DRAG
    right_side_east = east * ice_mass_per_area + DTE * (
        eastward_force + forcing[0] + ice_mass_per_area * coriolis_parameter * north
    )
    right_side_north = north * ice_mass_per_area + DTE * (
        northward_force + forcing[1] - ice_mass_per_area * coriolis_parameter * east
    )
    return jnp.stack(
        [
            velocity_mask * right_side_east / implicit_denominator,
            velocity_mask * right_side_north / implicit_denominator,
        ]
    )


def column_growth(
    thickness,
    velocity,
    ocean_temp,
    ocean_salt,
    ocean_current_east,
    ocean_current_north,
    air_temp,
    omask,
):
    freeze = -0.054 * (SREF + ocean_salt)
    rel_east = velocity[0] - ocean_current_east
    rel_north = velocity[1] - ocean_current_north
    speed = jnp.sqrt(rel_east * rel_east + rel_north * rel_north + 0.01)
    melt = GAMMA * (ocean_temp - freeze) * speed
    growth = KAPPA * (freeze - air_temp) / (thickness + 0.1)
    return omask * jnp.maximum(thickness + DTT * (growth - melt), 0.0)


def body(
    ocean_blocks,
    block_map,
    velocity,
    stress,
    thickness,
    area,
    wind,
    air_temp,
    ice_presence_mask,
    ocean_land_mask,
    fold_partner_column,
):
    ocean = regroup_local(ocean_blocks, block_map)
    ocean_temp = ocean[:, 0, :]
    ocean_salt = ocean[:, 1, :]
    ocean_current_east = ocean[:, 2, :]
    ocean_current_north = ocean[:, 3, :]
    hsum = jnp.sum(area * thickness, axis=0)
    conc = jnp.sum(area, axis=0)
    strength = PSTAR * hsum * jnp.exp(-CSTAR * (1.0 - conc))
    ice_mass_per_area = hsum + 0.2
    rows = velocity.shape[1]
    cols = velocity.shape[2]
    total_rows = rows * lax.axis_size("gy")
    velocity_mask = (ice_presence_mask * ocean_land_mask).astype(jnp.float32)
    omask = ocean_land_mask.astype(jnp.float32)
    fold_col = fold_partner_column[0] % (cols * lax.axis_size("gx"))
    fold_start = fold_col // cols
    fold_rest = fold_col % cols

    width = 2 * ITERS
    stack = jnp.concatenate(
        [
            velocity,
            stress,
            strength[None],
            ice_mass_per_area[None],
            wind + DRAG * jnp.stack([ocean_current_east, ocean_current_north]),
            velocity_mask[None],
        ],
        axis=0,
    )
    signs = jnp.array(
        [-1.0, -1.0, 1.0, 1.0, 1.0, 1.0, 1.0, -1.0, -1.0, 1.0], jnp.float32
    ).reshape(-1, 1, 1)
    ext = exchange(stack, width, signs, fold_start, fold_rest)
    grid_row = lax.axis_index("gy") * rows + jnp.arange(-width, rows + width, dtype=jnp.int32)
    true_row = jnp.where(grid_row > total_rows - 1, 2 * total_rows - 1 - grid_row, grid_row)
    coriolis_ext = (FCOR * (true_row.astype(jnp.float32) + 0.5) / float(total_rows))[:, None]
    inside_ext = (grid_row >= 0)[:, None]

    def rows_crop(x, n):
        return x if n == 0 else x[n : x.shape[0] - n]

    vel = ext[0:2]
    st = ext[2:5]
    st_radius = width
    for step in range(ITERS):
        radius = width - 2 * step
        e11, e22, e12 = compute_strain_rates(vel[0], vel[1])
        st = stress_update(
            crop(st, st_radius - (radius - 1)),
            e11,
            e22,
            e12,
            crop(ext[5], width - (radius - 1)),
        )
        st = jnp.where(rows_crop(inside_ext, width - (radius - 1)), st, 0.0)
        st_radius = radius - 1
        eastward_force, northward_force = stress_force(st)
        n = width - (radius - 2)
        vel = momentum_solve(
            crop(vel, 2),
            eastward_force,
            northward_force,
            crop(ext[7:9], n),
            crop(ext[6], n),
            rows_crop(coriolis_ext, n),
            crop(ext[9], n),
        )
        vel = jnp.where(rows_crop(inside_ext, n), vel, 0.0)
    velocity = vel
    stress = crop(st, st_radius)
    thickness_out = column_growth(
        thickness,
        velocity,
        ocean_temp,
        ocean_salt,
        ocean_current_east,
        ocean_current_north,
        air_temp,
        omask,
    )
    return (velocity, stress, thickness_out)


def solution(mesh):
    placed = (
        P("gy", None, "gx"),
        P("gy", "gx"),
        P(None, "gy", "gx"),
        P(None, "gy", "gx"),
        P(None, "gy", "gx"),
        P(None, "gy", "gx"),
        P(None, "gy", "gx"),
        P("gy", "gx"),
        P("gy", "gx"),
        P("gy", "gx"),
        P(),
    )
    return jax.shard_map(
        body,
        mesh=mesh,
        in_specs=placed,
        out_specs=(P(None, "gy", "gx"), P(None, "gy", "gx"), P(None, "gy", "gx")),
        check_vma=False,
    )
```

```python
import jax
import jax.numpy as jnp
from jax import lax
from jax.sharding import PartitionSpec as P

ITERS = 4


RELAX = 0.5
ECC2 = 4.0
DMIN2 = 0.01
PSTAR = 1.0
CSTAR = 5.0
DTE = 0.3
DRAG = 1.0
FCOR = 0.5
KAPPA = 0.5
GAMMA = 0.3
DTT = 0.5
SREF = 34.0


def shift_pairs(count, step, cyclic):
    pairs = [(i, i + step) for i in range(count) if 0 <= i + step < count]
    if cyclic:
        pairs = [(i, (i + step) % count) for i in range(count)]
    return pairs


def regroup_local(ocean_blocks, block_map):
    rows, fields, cols = ocean_blocks.shape
    peers = lax.axis_size("gx")
    group = max(2, rows // peers)
    count = rows // group
    target = block_map[:, 0]
    dest_dev = target[::group] // rows
    dest_row = (target % rows).reshape(count, group)
    chosen = dest_dev[None, :] == jnp.arange(peers, dtype=jnp.int32)[:, None]
    source = jnp.sum(jnp.where(chosen, jnp.arange(count, dtype=jnp.int32)[None, :] + 1, 0), axis=1) - 1
    source = jnp.where(source < 0, count, source)
    blocks = jnp.concatenate(
        [ocean_blocks.reshape(count, group * fields * cols), jnp.zeros((1, group * fields * cols), jnp.float32)],
        axis=0,
    )
    outgoing = jnp.take(blocks, source, axis=0)
    labels = jnp.sum(jnp.where(chosen[:, :, None], dest_row[None, :, :] + 1, 0), axis=1) - 1
    packed = jnp.concatenate([outgoing, labels.astype(jnp.float32)], axis=1)
    arrived = lax.all_to_all(packed, "gx", split_axis=0, concat_axis=0, tiled=True)
    flat = arrived[:, : group * fields * cols].reshape(peers * group, fields * cols)
    arrived_rows = arrived[:, group * fields * cols :].astype(jnp.int32).reshape(-1)
    hits = arrived_rows[None, :] == jnp.arange(rows, dtype=jnp.int32)[:, None]
    where_from = jnp.sum(
        jnp.where(hits, jnp.arange(peers * group, dtype=jnp.int32)[None, :], 0), axis=1
    )
    local = jnp.take(flat, where_from, axis=0)
    return local.reshape(rows, fields, cols)


def exchange(stack, width, signs, fold_start, fold_rest):
    ny = lax.axis_size("gy")
    nx = lax.axis_size("gx")
    w = width
    cols = stack.shape[-1]
    low = 4 if nx % 4 == 0 else 1
    a = fold_start // low
    b = fold_start % low
    top_row = (ny - 1) * nx
    both = ("gy", "gx")

    def on_top(target):
        return [(top_row + e, top_row + target(e) % nx) for e in range(nx)]

    def stage_one(aa):
        def run(top, west_in, east_in):
            mirrored = lax.ppermute(top, both, on_top(lambda e: low * aa - e))
            west = lax.ppermute(west_in, "gx", shift_pairs(nx, 1, True))
            east = lax.ppermute(east_in, "gx", shift_pairs(nx, -1, True))
            return mirrored, west, east

        return run

    mirrored, west, east = lax.switch(
        a,
        [stage_one(aa) for aa in range(nx // low)],
        stack[:, -w:, :],
        stack[:, :, -w:],
        stack[:, :, :w],
    )
    wide = jnp.concatenate([west, stack, east], axis=2)
    spans = ((-2, -1, 0), (-1, 0), (-1, 0, 1))
    span = jnp.where(fold_rest < w - 1, 0, jnp.where(fold_rest > cols - 1 - w, 2, 1))

    def stage_two(bb, ts):
        def run(y, south_in, north_in):
            parts = [
                lax.ppermute(y, both, on_top(lambda e, t=t: e + bb + t)) for t in ts
            ]
            parts += [jnp.zeros_like(y)] * (3 - len(ts))
            south = lax.ppermute(south_in, "gy", shift_pairs(ny, 1, False))
            north = lax.ppermute(north_in, "gy", shift_pairs(ny, -1, False))
            return tuple(parts), south, north

        return run

    parts, south, north = lax.switch(
        b * len(spans) + span,
        [stage_two(bb, ts) for bb in range(low) for ts in spans],
        mirrored,
        wide[:, -w:, :],
        wide[:, :w, :],
    )
    strip = jnp.concatenate(parts, axis=-1)
    lowest = jnp.where(span == 0, 2, 1)
    first = lowest * cols + fold_rest - (cols - 1) - w
    window = lax.dynamic_slice_in_dim(strip, first, cols + 2 * w, axis=2)
    folded = jnp.flip(window, axis=(1, 2)) * signs
    north = jnp.where(lax.axis_index("gy") == ny - 1, folded, north)
    return jnp.concatenate([south, wide, north], axis=1)


def crop(x, n):
    if n == 0:
        return x
    return x[..., n : x.shape[-2] - n, n : x.shape[-1] - n]


def compute_strain_rates(u_pad, v_pad):
    strain_rate_east = (u_pad[1:-1, 2:] - u_pad[1:-1, :-2]) * 0.5
    strain_rate_north = (v_pad[2:, 1:-1] - v_pad[:-2, 1:-1]) * 0.5
    strain_rate_shear = (
        u_pad[2:, 1:-1] - u_pad[:-2, 1:-1] + (v_pad[1:-1, 2:] - v_pad[1:-1, :-2])
    ) * 0.25
    return (strain_rate_east, strain_rate_north, strain_rate_shear)


def stress_update(old, strain_rate_east, strain_rate_north, strain_rate_shear, strength):
    divergence = strain_rate_east + strain_rate_north
    tension = strain_rate_east - strain_rate_north
    shear = 2.0 * strain_rate_shear
    delta = jnp.sqrt(divergence * divergence + (tension * tension + shear * shear) / ECC2 + DMIN2)
    zeta = strength / delta
    first = (old[0] + RELAX * (zeta * divergence - strength)) / (1.0 + RELAX)
    second = (old[1] + RELAX * zeta * tension / ECC2) / (1.0 + RELAX)
    third = (old[2] + RELAX * zeta * shear / (2.0 * ECC2)) / (1.0 + RELAX)
    return jnp.stack([first, second, third])


def stress_force(padded):
    normal_x = (padded[0] + padded[1]) * 0.5
    normal_y = (padded[0] - padded[1]) * 0.5
    shear = padded[2]
    eastward_force = (normal_x[1:-1, 2:] - normal_x[1:-1, :-2]) * 0.5 + (
        shear[2:, 1:-1] - shear[:-2, 1:-1]
    ) * 0.5
    northward_force = (shear[1:-1, 2:] - shear[1:-1, :-2]) * 0.5 + (
        normal_y[2:, 1:-1] - normal_y[:-2, 1:-1]
    ) * 0.5
    return (eastward_force, northward_force)


def momentum_solve(
    velocity,
    eastward_force,
    northward_force,
    forcing,
    ice_mass_per_area,
    coriolis_parameter,
    velocity_mask,
):
    east = velocity[0]
    north = velocity[1]
    implicit_denominator = ice_mass_per_area + DTE * DRAG
    right_side_east = east * ice_mass_per_area + DTE * (
        eastward_force + forcing[0] + ice_mass_per_area * coriolis_parameter * north
    )
    right_side_north = north * ice_mass_per_area + DTE * (
        northward_force + forcing[1] - ice_mass_per_area * coriolis_parameter * east
    )
    return jnp.stack(
        [
            velocity_mask * right_side_east / implicit_denominator,
            velocity_mask * right_side_north / implicit_denominator,
        ]
    )


def column_growth(
    thickness,
    velocity,
    ocean_temp,
    ocean_salt,
    ocean_current_east,
    ocean_current_north,
    air_temp,
    omask,
):
    freeze = -0.054 * (SREF + ocean_salt)
    rel_east = velocity[0] - ocean_current_east
    rel_north = velocity[1] - ocean_current_north
    speed = jnp.sqrt(rel_east * rel_east + rel_north * rel_north + 0.01)
    melt = GAMMA * (ocean_temp - freeze) * speed
    growth = KAPPA * (freeze - air_temp) / (thickness + 0.1)
    return omask * jnp.maximum(thickness + DTT * (growth - melt), 0.0)


def body(
    ocean_blocks,
    block_map,
    velocity,
    stress,
    thickness,
    area,
    wind,
    air_temp,
    ice_presence_mask,
    ocean_land_mask,
    fold_partner_column,
):
    ocean = regroup_local(ocean_blocks, block_map)
    ocean_temp = ocean[:, 0, :]
    ocean_salt = ocean[:, 1, :]
    ocean_current_east = ocean[:, 2, :]
    ocean_current_north = ocean[:, 3, :]
    hsum = jnp.sum(area * thickness, axis=0)
    conc = jnp.sum(area, axis=0)
    strength = PSTAR * hsum * jnp.exp(-CSTAR * (1.0 - conc))
    ice_mass_per_area = hsum + 0.2
    rows = velocity.shape[1]
    cols = velocity.shape[2]
    total_rows = rows * lax.axis_size("gy")
    velocity_mask = (ice_presence_mask * ocean_land_mask).astype(jnp.float32)
    omask = ocean_land_mask.astype(jnp.float32)
    fold_col = fold_partner_column[0] % (cols * lax.axis_size("gx"))
    fold_start = fold_col // cols
    fold_rest = fold_col % cols

    width = 2 * ITERS
    stack = jnp.concatenate(
        [
            velocity,
            stress,
            strength[None],
            ice_mass_per_area[None],
            wind + DRAG * jnp.stack([ocean_current_east, ocean_current_north]),
            velocity_mask[None],
        ],
        axis=0,
    )
    signs = jnp.array(
        [-1.0, -1.0, 1.0, 1.0, 1.0, 1.0, 1.0, -1.0, -1.0, 1.0], jnp.float32
    ).reshape(-1, 1, 1)
    ext = exchange(stack, width, signs, fold_start, fold_rest)
    grid_row = lax.axis_index("gy") * rows + jnp.arange(-width, rows + width, dtype=jnp.int32)
    true_row = jnp.where(grid_row > total_rows - 1, 2 * total_rows - 1 - grid_row, grid_row)
    coriolis_ext = (FCOR * (true_row.astype(jnp.float32) + 0.5) / float(total_rows))[:, None]
    inside_ext = (grid_row >= 0)[:, None]

    def rows_crop(x, n):
        return x if n == 0 else x[n : x.shape[0] - n]

    vel = ext[0:2]
    st = ext[2:5]
    st_radius = width
    for step in range(ITERS):
        radius = width - 2 * step
        e11, e22, e12 = compute_strain_rates(vel[0], vel[1])
        st = stress_update(
            crop(st, st_radius - (radius - 1)),
            e11,
            e22,
            e12,
            crop(ext[5], width - (radius - 1)),
        )
        st = jnp.where(rows_crop(inside_ext, width - (radius - 1)), st, 0.0)
        st_radius = radius - 1
        eastward_force, northward_force = stress_force(st)
        n = width - (radius - 2)
        vel = momentum_solve(
            crop(vel, 2),
            eastward_force,
            northward_force,
            crop(ext[7:9], n),
            crop(ext[6], n),
            rows_crop(coriolis_ext, n),
            crop(ext[9], n),
        )
        vel = jnp.where(rows_crop(inside_ext, n), vel, 0.0)
    velocity = vel
    stress = crop(st, st_radius)
    thickness_out = column_growth(
        thickness,
        velocity,
        ocean_temp,
        ocean_salt,
        ocean_current_east,
        ocean_current_north,
        air_temp,
        omask,
    )
    return (velocity, stress, thickness_out)


def solution(mesh):
    placed = (
        P("gy", None, "gx"),
        P("gy", "gx"),
        P(None, "gy", "gx"),
        P(None, "gy", "gx"),
        P(None, "gy", "gx"),
        P(None, "gy", "gx"),
        P(None, "gy", "gx"),
        P("gy", "gx"),
        P("gy", "gx"),
        P("gy", "gx"),
        P(),
    )
    return jax.shard_map(
        body,
        mesh=mesh,
        in_specs=placed,
        out_specs=(P(None, "gy", "gx"), P(None, "gy", "gx"), P(None, "gy", "gx")),
        check_vma=False,
    )
```

```python
import jax
import jax.numpy as jnp
from jax import lax
from jax.sharding import PartitionSpec as P

ITERS = 4


RELAX = 0.5
ECC2 = 4.0
DMIN2 = 0.01
PSTAR = 1.0
CSTAR = 5.0
DTE = 0.3
DRAG = 1.0
FCOR = 0.5
KAPPA = 0.5
GAMMA = 0.3
DTT = 0.5
SREF = 34.0


def shift_pairs(count, step, cyclic):
    pairs = [(i, i + step) for i in range(count) if 0 <= i + step < count]
    if cyclic:
        pairs = [(i, (i + step) % count) for i in range(count)]
    return pairs


def regroup_local(ocean_blocks, block_map):
    rows, fields, cols = ocean_blocks.shape
    peers = lax.axis_size("gx")
    group = max(2, rows // peers)
    count = rows // group
    target = block_map[:, 0]
    dest_dev = target[::group] // rows
    dest_row = (target % rows).reshape(count, group)
    chosen = dest_dev[None, :] == jnp.arange(peers, dtype=jnp.int32)[:, None]
    blocks = ocean_blocks.reshape(count, group * fields * cols)
    outgoing = jnp.dot(
        chosen.astype(jnp.float32),
        blocks,
        precision=lax.Precision.HIGHEST,
        preferred_element_type=jnp.float32,
    )
    labels = jnp.sum(jnp.where(chosen[:, :, None], dest_row[None, :, :] + 1, 0), axis=1) - 1
    packed = jnp.concatenate([outgoing, labels.astype(jnp.float32)], axis=1)
    arrived = lax.all_to_all(packed, "gx", split_axis=0, concat_axis=0, tiled=True)
    flat = arrived[:, : group * fields * cols].reshape(peers * group, fields * cols)
    arrived_rows = arrived[:, group * fields * cols :].astype(jnp.int32)
    hits = arrived_rows.reshape(-1)[None, :] == jnp.arange(rows, dtype=jnp.int32)[:, None]
    where_from = jnp.sum(
        jnp.where(hits, jnp.arange(peers * group, dtype=jnp.int32)[None, :], 0), axis=1
    )
    local = jnp.take(flat, where_from, axis=0)
    return local.reshape(rows, fields, cols)


def exchange(stack, width, signs, fold_start, fold_rest):
    ny = lax.axis_size("gy")
    nx = lax.axis_size("gx")
    w = width
    cols = stack.shape[-1]
    low = 4 if nx % 4 == 0 else 1
    a = fold_start // low
    b = fold_start % low
    top_row = (ny - 1) * nx
    both = ("gy", "gx")

    def on_top(target):
        return [(top_row + e, top_row + target(e) % nx) for e in range(nx)]

    def stage_one(aa):
        def run(top, west_in, east_in):
            mirrored = lax.ppermute(top, both, on_top(lambda e: low * aa - e))
            west = lax.ppermute(west_in, "gx", shift_pairs(nx, 1, True))
            east = lax.ppermute(east_in, "gx", shift_pairs(nx, -1, True))
            return mirrored, west, east

        return run

    mirrored, west, east = lax.switch(
        a,
        [stage_one(aa) for aa in range(nx // low)],
        stack[:, -w:, :],
        stack[:, :, -w:],
        stack[:, :, :w],
    )
    wide = jnp.concatenate([west, stack, east], axis=2)
    spans = ((-2, -1, 0), (-1, 0), (-1, 0, 1))
    span = jnp.where(fold_rest < w - 1, 0, jnp.where(fold_rest > cols - 1 - w, 2, 1))

    def stage_two(bb, ts):
        def run(y, south_in, north_in):
            parts = [
                lax.ppermute(y, both, on_top(lambda e, t=t: e + bb + t)) for t in ts
            ]
            parts += [jnp.zeros_like(y)] * (3 - len(ts))
            south = lax.ppermute(south_in, "gy", shift_pairs(ny, 1, False))
            north = lax.ppermute(north_in, "gy", shift_pairs(ny, -1, False))
            return tuple(parts), south, north

        return run

    parts, south, north = lax.switch(
        b * len(spans) + span,
        [stage_two(bb, ts) for bb in range(low) for ts in spans],
        mirrored,
        wide[:, -w:, :],
        wide[:, :w, :],
    )
    strip = jnp.concatenate(parts, axis=-1)
    lowest = jnp.where(span == 0, 2, 1)
    first = lowest * cols + fold_rest - (cols - 1) - w
    window = lax.dynamic_slice_in_dim(strip, first, cols + 2 * w, axis=2)
    folded = jnp.flip(window, axis=(1, 2)) * signs
    north = jnp.where(lax.axis_index("gy") == ny - 1, folded, north)
    return jnp.concatenate([south, wide, north], axis=1)


def crop(x, n):
    if n == 0:
        return x
    return x[..., n : x.shape[-2] - n, n : x.shape[-1] - n]


def compute_strain_rates(u_pad, v_pad):
    strain_rate_east = (u_pad[1:-1, 2:] - u_pad[1:-1, :-2]) * 0.5
    strain_rate_north = (v_pad[2:, 1:-1] - v_pad[:-2, 1:-1]) * 0.5
    strain_rate_shear = (
        u_pad[2:, 1:-1] - u_pad[:-2, 1:-1] + (v_pad[1:-1, 2:] - v_pad[1:-1, :-2])
    ) * 0.25
    return (strain_rate_east, strain_rate_north, strain_rate_shear)


def stress_update(old, strain_rate_east, strain_rate_north, strain_rate_shear, strength):
    divergence = strain_rate_east + strain_rate_north
    tension = strain_rate_east - strain_rate_north
    shear = 2.0 * strain_rate_shear
    delta = jnp.sqrt(divergence * divergence + (tension * tension + shear * shear) / ECC2 + DMIN2)
    zeta = strength / delta
    first = (old[0] + RELAX * (zeta * divergence - strength)) / (1.0 + RELAX)
    second = (old[1] + RELAX * zeta * tension / ECC2) / (1.0 + RELAX)
    third = (old[2] + RELAX * zeta * shear / (2.0 * ECC2)) / (1.0 + RELAX)
    return jnp.stack([first, second, third])


def stress_force(padded):
    normal_x = (padded[0] + padded[1]) * 0.5
    normal_y = (padded[0] - padded[1]) * 0.5
    shear = padded[2]
    eastward_force = (normal_x[1:-1, 2:] - normal_x[1:-1, :-2]) * 0.5 + (
        shear[2:, 1:-1] - shear[:-2, 1:-1]
    ) * 0.5
    northward_force = (shear[1:-1, 2:] - shear[1:-1, :-2]) * 0.5 + (
        normal_y[2:, 1:-1] - normal_y[:-2, 1:-1]
    ) * 0.5
    return (eastward_force, northward_force)


def momentum_solve(
    velocity,
    eastward_force,
    northward_force,
    forcing,
    ice_mass_per_area,
    coriolis_parameter,
    velocity_mask,
):
    east = velocity[0]
    north = velocity[1]
    implicit_denominator = ice_mass_per_area + DTE * DRAG
    right_side_east = east * ice_mass_per_area + DTE * (
        eastward_force + forcing[0] + ice_mass_per_area * coriolis_parameter * north
    )
    right_side_north = north * ice_mass_per_area + DTE * (
        northward_force + forcing[1] - ice_mass_per_area * coriolis_parameter * east
    )
    return jnp.stack(
        [
            velocity_mask * right_side_east / implicit_denominator,
            velocity_mask * right_side_north / implicit_denominator,
        ]
    )


def column_growth(
    thickness,
    velocity,
    ocean_temp,
    ocean_salt,
    ocean_current_east,
    ocean_current_north,
    air_temp,
    omask,
):
    freeze = -0.054 * (SREF + ocean_salt)
    rel_east = velocity[0] - ocean_current_east
    rel_north = velocity[1] - ocean_current_north
    speed = jnp.sqrt(rel_east * rel_east + rel_north * rel_north + 0.01)
    melt = GAMMA * (ocean_temp - freeze) * speed
    growth = KAPPA * (freeze - air_temp) / (thickness + 0.1)
    return omask * jnp.maximum(thickness + DTT * (growth - melt), 0.0)


def body(
    ocean_blocks,
    block_map,
    velocity,
    stress,
    thickness,
    area,
    wind,
    air_temp,
    ice_presence_mask,
    ocean_land_mask,
    fold_partner_column,
):
    ocean = regroup_local(ocean_blocks, block_map)
    ocean_temp = ocean[:, 0, :]
    ocean_salt = ocean[:, 1, :]
    ocean_current_east = ocean[:, 2, :]
    ocean_current_north = ocean[:, 3, :]
    hsum = jnp.sum(area * thickness, axis=0)
    conc = jnp.sum(area, axis=0)
    strength = PSTAR * hsum * jnp.exp(-CSTAR * (1.0 - conc))
    ice_mass_per_area = hsum + 0.2
    rows = velocity.shape[1]
    cols = velocity.shape[2]
    total_rows = rows * lax.axis_size("gy")
    velocity_mask = (ice_presence_mask * ocean_land_mask).astype(jnp.float32)
    omask = ocean_land_mask.astype(jnp.float32)
    fold_col = fold_partner_column[0] % (cols * lax.axis_size("gx"))
    fold_start = fold_col // cols
    fold_rest = fold_col % cols

    width = 2 * ITERS
    stack = jnp.concatenate(
        [
            velocity,
            stress,
            strength[None],
            ice_mass_per_area[None],
            wind + DRAG * jnp.stack([ocean_current_east, ocean_current_north]),
            velocity_mask[None],
        ],
        axis=0,
    )
    signs = jnp.array(
        [-1.0, -1.0, 1.0, 1.0, 1.0, 1.0, 1.0, -1.0, -1.0, 1.0], jnp.float32
    ).reshape(-1, 1, 1)
    ext = exchange(stack, width, signs, fold_start, fold_rest)
    grid_row = lax.axis_index("gy") * rows + jnp.arange(-width, rows + width, dtype=jnp.int32)
    true_row = jnp.where(grid_row > total_rows - 1, 2 * total_rows - 1 - grid_row, grid_row)
    coriolis_ext = (FCOR * (true_row.astype(jnp.float32) + 0.5) / float(total_rows))[:, None]
    inside_ext = (grid_row >= 0)[:, None]

    def rows_crop(x, n):
        return x if n == 0 else x[n : x.shape[0] - n]

    vel = ext[0:2]
    st = ext[2:5]
    st_radius = width
    for step in range(ITERS):
        radius = width - 2 * step
        e11, e22, e12 = compute_strain_rates(vel[0], vel[1])
        st = stress_update(
            crop(st, st_radius - (radius - 1)),
            e11,
            e22,
            e12,
            crop(ext[5], width - (radius - 1)),
        )
        st = jnp.where(rows_crop(inside_ext, width - (radius - 1)), st, 0.0)
        st_radius = radius - 1
        eastward_force, northward_force = stress_force(st)
        n = width - (radius - 2)
        vel = momentum_solve(
            crop(vel, 2),
            eastward_force,
            northward_force,
            crop(ext[7:9], n),
            crop(ext[6], n),
            rows_crop(coriolis_ext, n),
            crop(ext[9], n),
        )
        vel = jnp.where(rows_crop(inside_ext, n), vel, 0.0)
    velocity = vel
    stress = crop(st, st_radius)
    thickness_out = column_growth(
        thickness,
        velocity,
        ocean_temp,
        ocean_salt,
        ocean_current_east,
        ocean_current_north,
        air_temp,
        omask,
    )
    return (velocity, stress, thickness_out)


def solution(mesh):
    placed = (
        P("gy", None, "gx"),
        P("gy", "gx"),
        P(None, "gy", "gx"),
        P(None, "gy", "gx"),
        P(None, "gy", "gx"),
        P(None, "gy", "gx"),
        P(None, "gy", "gx"),
        P("gy", "gx"),
        P("gy", "gx"),
        P("gy", "gx"),
        P(),
    )
    return jax.shard_map(
        body,
        mesh=mesh,
        in_specs=placed,
        out_specs=(P(None, "gy", "gx"), P(None, "gy", "gx"), P(None, "gy", "gx")),
        check_vma=False,
    )
```

```python
import jax
import jax.numpy as jnp
from jax import lax
from jax.sharding import PartitionSpec as P

ITERS = 4


RELAX = 0.5
ECC2 = 4.0
DMIN2 = 0.01
PSTAR = 1.0
CSTAR = 5.0
DTE = 0.3
DRAG = 1.0
FCOR = 0.5
KAPPA = 0.5
GAMMA = 0.3
DTT = 0.5
SREF = 34.0


def shift_pairs(count, step, cyclic):
    pairs = [(i, i + step) for i in range(count) if 0 <= i + step < count]
    if cyclic:
        pairs = [(i, (i + step) % count) for i in range(count)]
    return pairs


def regroup_local(ocean_blocks, block_map):
    rows, fields, cols = ocean_blocks.shape
    peers = lax.axis_size("gx")
    group = max(2, rows // peers)
    count = rows // group
    target = block_map[:, 0]
    dest_dev = target[::group] // rows
    dest_row = (target % rows).reshape(count, group)
    chosen = dest_dev[None, :] == jnp.arange(peers, dtype=jnp.int32)[:, None]
    blocks = ocean_blocks.reshape(count, group * fields * cols)
    outgoing = jnp.dot(
        chosen.astype(jnp.float32),
        blocks,
        precision=lax.Precision.HIGHEST,
        preferred_element_type=jnp.float32,
    )
    labels = jnp.sum(jnp.where(chosen[:, :, None], dest_row[None, :, :] + 1, 0), axis=1) - 1
    packed = jnp.concatenate([outgoing, labels.astype(jnp.float32)], axis=1)
    arrived = lax.all_to_all(packed, "gx", split_axis=0, concat_axis=0, tiled=True)
    flat = arrived[:, : group * fields * cols].reshape(peers * group, fields * cols)
    arrived_rows = arrived[:, group * fields * cols :].astype(jnp.int32)
    picks = (
        arrived_rows.reshape(-1)[None, :] == jnp.arange(rows, dtype=jnp.int32)[:, None]
    ).astype(jnp.float32)
    local = jnp.dot(
        picks, flat, precision=lax.Precision.HIGHEST, preferred_element_type=jnp.float32
    )
    return local.reshape(rows, fields, cols)


def exchange(stack, width, signs, fold_start, fold_rest):
    ny = lax.axis_size("gy")
    nx = lax.axis_size("gx")
    w = width
    cols = stack.shape[-1]
    low = 4 if nx % 4 == 0 else 1
    a = fold_start // low
    b = fold_start % low
    top_row = (ny - 1) * nx
    both = ("gy", "gx")

    def on_top(target):
        return [(top_row + e, top_row + target(e) % nx) for e in range(nx)]

    def stage_one(aa):
        def run(top, west_in, east_in):
            mirrored = lax.ppermute(top, both, on_top(lambda e: low * aa - e))
            west = lax.ppermute(west_in, "gx", shift_pairs(nx, 1, True))
            east = lax.ppermute(east_in, "gx", shift_pairs(nx, -1, True))
            return mirrored, west, east

        return run

    mirrored, west, east = lax.switch(
        a,
        [stage_one(aa) for aa in range(nx // low)],
        stack[:, -w:, :] * signs,
        stack[:, :, -w:],
        stack[:, :, :w],
    )
    wide = jnp.concatenate([west, stack, east], axis=2)
    spans = ((-2, -1, 0), (-1, 0), (-1, 0, 1))
    span = jnp.where(fold_rest < w - 1, 0, jnp.where(fold_rest > cols - 1 - w, 2, 1))

    def stage_two(bb, ts):
        def run(y, south_in, north_in):
            parts = [
                lax.ppermute(y, both, on_top(lambda e, t=t: e + bb + t)) for t in ts
            ]
            parts += [jnp.zeros_like(y)] * (3 - len(ts))
            south = lax.ppermute(south_in, "gy", shift_pairs(ny, 1, False))
            north = lax.ppermute(north_in, "gy", shift_pairs(ny, -1, False))
            return tuple(parts), south, north

        return run

    parts, south, north = lax.switch(
        b * len(spans) + span,
        [stage_two(bb, ts) for bb in range(low) for ts in spans],
        mirrored,
        wide[:, -w:, :],
        wide[:, :w, :],
    )
    strip = jnp.concatenate(parts, axis=-1)
    lowest = jnp.where(span == 0, 2, 1)
    first = lowest * cols + fold_rest - (cols - 1) - w
    window = lax.dynamic_slice_in_dim(strip, first, cols + 2 * w, axis=2)
    folded = jnp.flip(window, axis=(1, 2))
    north = jnp.where(lax.axis_index("gy") == ny - 1, folded, north)
    return jnp.concatenate([south, wide, north], axis=1)


def crop(x, n):
    if n == 0:
        return x
    return x[..., n : x.shape[-2] - n, n : x.shape[-1] - n]


def compute_strain_rates(u_pad, v_pad):
    strain_rate_east = (u_pad[1:-1, 2:] - u_pad[1:-1, :-2]) * 0.5
    strain_rate_north = (v_pad[2:, 1:-1] - v_pad[:-2, 1:-1]) * 0.5
    strain_rate_shear = (
        u_pad[2:, 1:-1] - u_pad[:-2, 1:-1] + (v_pad[1:-1, 2:] - v_pad[1:-1, :-2])
    ) * 0.25
    return (strain_rate_east, strain_rate_north, strain_rate_shear)


def stress_update(old, strain_rate_east, strain_rate_north, strain_rate_shear, strength):
    divergence = strain_rate_east + strain_rate_north
    tension = strain_rate_east - strain_rate_north
    shear = 2.0 * strain_rate_shear
    delta = jnp.sqrt(divergence * divergence + (tension * tension + shear * shear) / ECC2 + DMIN2)
    zeta = strength / delta
    first = (old[0] + RELAX * (zeta * divergence - strength)) / (1.0 + RELAX)
    second = (old[1] + RELAX * zeta * tension / ECC2) / (1.0 + RELAX)
    third = (old[2] + RELAX * zeta * shear / (2.0 * ECC2)) / (1.0 + RELAX)
    return jnp.stack([first, second, third])


def stress_force(padded):
    normal_x = (padded[0] + padded[1]) * 0.5
    normal_y = (padded[0] - padded[1]) * 0.5
    shear = padded[2]
    eastward_force = (normal_x[1:-1, 2:] - normal_x[1:-1, :-2]) * 0.5 + (
        shear[2:, 1:-1] - shear[:-2, 1:-1]
    ) * 0.5
    northward_force = (shear[1:-1, 2:] - shear[1:-1, :-2]) * 0.5 + (
        normal_y[2:, 1:-1] - normal_y[:-2, 1:-1]
    ) * 0.5
    return (eastward_force, northward_force)


def momentum_solve(
    velocity,
    eastward_force,
    northward_force,
    forcing,
    ice_mass_per_area,
    coriolis_parameter,
    velocity_mask,
):
    east = velocity[0]
    north = velocity[1]
    implicit_denominator = ice_mass_per_area + DTE * DRAG
    right_side_east = east * ice_mass_per_area + DTE * (
        eastward_force + forcing[0] + ice_mass_per_area * coriolis_parameter * north
    )
    right_side_north = north * ice_mass_per_area + DTE * (
        northward_force + forcing[1] - ice_mass_per_area * coriolis_parameter * east
    )
    return jnp.stack(
        [
            velocity_mask * right_side_east / implicit_denominator,
            velocity_mask * right_side_north / implicit_denominator,
        ]
    )


def column_growth(
    thickness,
    velocity,
    ocean_temp,
    ocean_salt,
    ocean_current_east,
    ocean_current_north,
    air_temp,
    omask,
):
    freeze = -0.054 * (SREF + ocean_salt)
    rel_east = velocity[0] - ocean_current_east
    rel_north = velocity[1] - ocean_current_north
    speed = jnp.sqrt(rel_east * rel_east + rel_north * rel_north + 0.01)
    melt = GAMMA * (ocean_temp - freeze) * speed
    growth = KAPPA * (freeze - air_temp) / (thickness + 0.1)
    return omask * jnp.maximum(thickness + DTT * (growth - melt), 0.0)


def body(
    ocean_blocks,
    block_map,
    velocity,
    stress,
    thickness,
    area,
    wind,
    air_temp,
    ice_presence_mask,
    ocean_land_mask,
    fold_partner_column,
):
    ocean = regroup_local(ocean_blocks, block_map)
    ocean_temp = ocean[:, 0, :]
    ocean_salt = ocean[:, 1, :]
    ocean_current_east = ocean[:, 2, :]
    ocean_current_north = ocean[:, 3, :]
    hsum = jnp.sum(area * thickness, axis=0)
    conc = jnp.sum(area, axis=0)
    strength = PSTAR * hsum * jnp.exp(-CSTAR * (1.0 - conc))
    ice_mass_per_area = hsum + 0.2
    rows = velocity.shape[1]
    cols = velocity.shape[2]
    total_rows = rows * lax.axis_size("gy")
    velocity_mask = (ice_presence_mask * ocean_land_mask).astype(jnp.float32)
    omask = ocean_land_mask.astype(jnp.float32)
    fold_col = fold_partner_column[0] % (cols * lax.axis_size("gx"))
    fold_start = fold_col // cols
    fold_rest = fold_col % cols

    width = 2 * ITERS
    stack = jnp.concatenate(
        [
            velocity,
            stress,
            strength[None],
            ice_mass_per_area[None],
            wind + DRAG * jnp.stack([ocean_current_east, ocean_current_north]),
            velocity_mask[None],
        ],
        axis=0,
    )
    signs = jnp.array(
        [-1.0, -1.0, 1.0, 1.0, 1.0, 1.0, 1.0, -1.0, -1.0, 1.0], jnp.float32
    ).reshape(-1, 1, 1)
    ext = exchange(stack, width, signs, fold_start, fold_rest)
    grid_row = lax.axis_index("gy") * rows + jnp.arange(-width, rows + width, dtype=jnp.int32)
    true_row = jnp.where(grid_row > total_rows - 1, 2 * total_rows - 1 - grid_row, grid_row)
    coriolis_ext = (FCOR * (true_row.astype(jnp.float32) + 0.5) / float(total_rows))[:, None]
    inside_ext = (grid_row >= 0)[:, None]

    def rows_crop(x, n):
        return x if n == 0 else x[n : x.shape[0] - n]

    vel = ext[0:2]
    st = ext[2:5]
    st_radius = width
    for step in range(ITERS):
        radius = width - 2 * step
        e11, e22, e12 = compute_strain_rates(vel[0], vel[1])
        st = stress_update(
            crop(st, st_radius - (radius - 1)),
            e11,
            e22,
            e12,
            crop(ext[5], width - (radius - 1)),
        )
        st = jnp.where(rows_crop(inside_ext, width - (radius - 1)), st, 0.0)
        st_radius = radius - 1
        eastward_force, northward_force = stress_force(st)
        n = width - (radius - 2)
        vel = momentum_solve(
            crop(vel, 2),
            eastward_force,
            northward_force,
            crop(ext[7:9], n),
            crop(ext[6], n),
            rows_crop(coriolis_ext, n),
            crop(ext[9], n),
        )
        vel = jnp.where(rows_crop(inside_ext, n), vel, 0.0)
    velocity = vel
    stress = crop(st, st_radius)
    thickness_out = column_growth(
        thickness,
        velocity,
        ocean_temp,
        ocean_salt,
        ocean_current_east,
        ocean_current_north,
        air_temp,
        omask,
    )
    return (velocity, stress, thickness_out)


def solution(mesh):
    placed = (
        P("gy", None, "gx"),
        P("gy", "gx"),
        P(None, "gy", "gx"),
        P(None, "gy", "gx"),
        P(None, "gy", "gx"),
        P(None, "gy", "gx"),
        P(None, "gy", "gx"),
        P("gy", "gx"),
        P("gy", "gx"),
        P("gy", "gx"),
        P(),
    )
    return jax.shard_map(
        body,
        mesh=mesh,
        in_specs=placed,
        out_specs=(P(None, "gy", "gx"), P(None, "gy", "gx"), P(None, "gy", "gx")),
        check_vma=False,
    )
```

```python
import jax
import jax.numpy as jnp
from jax import lax
from jax.sharding import PartitionSpec as P

ITERS = 4


RELAX = 0.5
ECC2 = 4.0
DMIN2 = 0.01
PSTAR = 1.0
CSTAR = 5.0
DTE = 0.3
DRAG = 1.0
FCOR = 0.5
KAPPA = 0.5
GAMMA = 0.3
DTT = 0.5
SREF = 34.0


def shift_pairs(count, step, cyclic):
    pairs = [(i, i + step) for i in range(count) if 0 <= i + step < count]
    if cyclic:
        pairs = [(i, (i + step) % count) for i in range(count)]
    return pairs


def regroup_local(ocean_blocks, block_map):
    rows, fields, cols = ocean_blocks.shape
    peers = lax.axis_size("gx")
    group = max(2, rows // peers)
    count = rows // group
    target = block_map[:, 0]
    dest_dev = target[::group] // rows
    dest_row = (target % rows).reshape(count, group)
    chosen = dest_dev[None, :] == jnp.arange(peers, dtype=jnp.int32)[:, None]
    blocks = ocean_blocks.reshape(count, group * fields * cols)
    outgoing = jnp.dot(
        chosen.astype(jnp.float32),
        blocks,
        precision=lax.Precision.HIGHEST,
        preferred_element_type=jnp.float32,
    )
    labels = jnp.sum(jnp.where(chosen[:, :, None], dest_row[None, :, :] + 1, 0), axis=1) - 1
    packed = jnp.concatenate([outgoing, labels.astype(jnp.float32)], axis=1)
    arrived = lax.all_to_all(packed, "gx", split_axis=0, concat_axis=0, tiled=True)
    flat = arrived[:, : group * fields * cols].reshape(peers * group, fields * cols)
    arrived_rows = arrived[:, group * fields * cols :].astype(jnp.int32)
    hits = arrived_rows.reshape(-1)[None, :] == jnp.arange(rows, dtype=jnp.int32)[:, None]
    where_from = jnp.sum(
        jnp.where(hits, jnp.arange(peers * group, dtype=jnp.int32)[None, :], 0), axis=1
    )
    local = jnp.take(flat, where_from, axis=0)
    return local.reshape(rows, fields, cols)


def exchange(stack, width, signs, fold_start, fold_rest):
    ny = lax.axis_size("gy")
    nx = lax.axis_size("gx")
    w = width
    cols = stack.shape[-1]
    low = 4 if nx % 4 == 0 else 1
    a = fold_start // low
    b = fold_start % low
    top_row = (ny - 1) * nx
    both = ("gy", "gx")

    def on_top(target):
        return [(top_row + e, top_row + target(e) % nx) for e in range(nx)]

    def stage_one(aa):
        def run(top, west_in, east_in):
            mirrored = lax.ppermute(top, both, on_top(lambda e: low * aa - e))
            west = lax.ppermute(west_in, "gx", shift_pairs(nx, 1, True))
            east = lax.ppermute(east_in, "gx", shift_pairs(nx, -1, True))
            return mirrored, west, east

        return run

    mirrored, west, east = lax.switch(
        a,
        [stage_one(aa) for aa in range(nx // low)],
        stack[:, -w:, :] * signs,
        stack[:, :, -w:],
        stack[:, :, :w],
    )
    wide = jnp.concatenate([west, stack, east], axis=2)
    spans = ((-2, -1, 0), (-1, 0), (-1, 0, 1))
    span = jnp.where(fold_rest < w - 1, 0, jnp.where(fold_rest > cols - 1 - w, 2, 1))

    def stage_two(bb, ts):
        def run(y, south_in, north_in):
            parts = [
                lax.ppermute(y, both, on_top(lambda e, t=t: e + bb + t)) for t in ts
            ]
            parts += [jnp.zeros_like(y)] * (3 - len(ts))
            south = lax.ppermute(south_in, "gy", shift_pairs(ny, 1, False))
            north = lax.ppermute(north_in, "gy", shift_pairs(ny, -1, False))
            return tuple(parts), south, north

        return run

    parts, south, north = lax.switch(
        b * len(spans) + span,
        [stage_two(bb, ts) for bb in range(low) for ts in spans],
        mirrored,
        wide[:, -w:, :],
        wide[:, :w, :],
    )
    strip = jnp.concatenate(parts, axis=-1)
    lowest = jnp.where(span == 0, 2, 1)
    first = lowest * cols + fold_rest - (cols - 1) - w
    window = lax.dynamic_slice_in_dim(strip, first, cols + 2 * w, axis=2)
    folded = jnp.flip(window, axis=(1, 2))
    north = jnp.where(lax.axis_index("gy") == ny - 1, folded, north)
    return jnp.concatenate([south, wide, north], axis=1)


def crop(x, n):
    if n == 0:
        return x
    return x[..., n : x.shape[-2] - n, n : x.shape[-1] - n]


def compute_strain_rates(u_pad, v_pad):
    strain_rate_east = (u_pad[1:-1, 2:] - u_pad[1:-1, :-2]) * 0.5
    strain_rate_north = (v_pad[2:, 1:-1] - v_pad[:-2, 1:-1]) * 0.5
    strain_rate_shear = (
        u_pad[2:, 1:-1] - u_pad[:-2, 1:-1] + (v_pad[1:-1, 2:] - v_pad[1:-1, :-2])
    ) * 0.25
    return (strain_rate_east, strain_rate_north, strain_rate_shear)


def stress_update(old, strain_rate_east, strain_rate_north, strain_rate_shear, strength):
    divergence = strain_rate_east + strain_rate_north
    tension = strain_rate_east - strain_rate_north
    shear = 2.0 * strain_rate_shear
    delta = jnp.sqrt(divergence * divergence + (tension * tension + shear * shear) / ECC2 + DMIN2)
    zeta = strength / delta
    first = (old[0] + RELAX * (zeta * divergence - strength)) / (1.0 + RELAX)
    second = (old[1] + RELAX * zeta * tension / ECC2) / (1.0 + RELAX)
    third = (old[2] + RELAX * zeta * shear / (2.0 * ECC2)) / (1.0 + RELAX)
    return jnp.stack([first, second, third])


def stress_force(padded):
    normal_x = (padded[0] + padded[1]) * 0.5
    normal_y = (padded[0] - padded[1]) * 0.5
    shear = padded[2]
    eastward_force = (normal_x[1:-1, 2:] - normal_x[1:-1, :-2]) * 0.5 + (
        shear[2:, 1:-1] - shear[:-2, 1:-1]
    ) * 0.5
    northward_force = (shear[1:-1, 2:] - shear[1:-1, :-2]) * 0.5 + (
        normal_y[2:, 1:-1] - normal_y[:-2, 1:-1]
    ) * 0.5
    return (eastward_force, northward_force)


def momentum_solve(
    velocity,
    eastward_force,
    northward_force,
    forcing,
    ice_mass_per_area,
    coriolis_parameter,
    velocity_mask,
):
    east = velocity[0]
    north = velocity[1]
    implicit_denominator = ice_mass_per_area + DTE * DRAG
    right_side_east = east * ice_mass_per_area + DTE * (
        eastward_force + forcing[0] + ice_mass_per_area * coriolis_parameter * north
    )
    right_side_north = north * ice_mass_per_area + DTE * (
        northward_force + forcing[1] - ice_mass_per_area * coriolis_parameter * east
    )
    return jnp.stack(
        [
            velocity_mask * right_side_east / implicit_denominator,
            velocity_mask * right_side_north / implicit_denominator,
        ]
    )


def column_growth(
    thickness,
    velocity,
    ocean_temp,
    ocean_salt,
    ocean_current_east,
    ocean_current_north,
    air_temp,
    omask,
):
    freeze = -0.054 * (SREF + ocean_salt)
    rel_east = velocity[0] - ocean_current_east
    rel_north = velocity[1] - ocean_current_north
    speed = jnp.sqrt(rel_east * rel_east + rel_north * rel_north + 0.01)
    melt = GAMMA * (ocean_temp - freeze) * speed
    growth = KAPPA * (freeze - air_temp) / (thickness + 0.1)
    return omask * jnp.maximum(thickness + DTT * (growth - melt), 0.0)


def body(
    ocean_blocks,
    block_map,
    velocity,
    stress,
    thickness,
    area,
    wind,
    air_temp,
    ice_presence_mask,
    ocean_land_mask,
    fold_partner_column,
):
    ocean = regroup_local(ocean_blocks, block_map)
    ocean_temp = ocean[:, 0, :]
    ocean_salt = ocean[:, 1, :]
    ocean_current_east = ocean[:, 2, :]
    ocean_current_north = ocean[:, 3, :]
    hsum = jnp.sum(area * thickness, axis=0)
    conc = jnp.sum(area, axis=0)
    strength = PSTAR * hsum * jnp.exp(-CSTAR * (1.0 - conc))
    ice_mass_per_area = hsum + 0.2
    rows = velocity.shape[1]
    cols = velocity.shape[2]
    total_rows = rows * lax.axis_size("gy")
    velocity_mask = (ice_presence_mask * ocean_land_mask).astype(jnp.float32)
    omask = ocean_land_mask.astype(jnp.float32)
    fold_col = fold_partner_column[0] % (cols * lax.axis_size("gx"))
    fold_start = fold_col // cols
    fold_rest = fold_col % cols

    width = 2 * ITERS
    stack = jnp.concatenate(
        [
            velocity,
            stress,
            strength[None],
            ice_mass_per_area[None],
            wind + DRAG * jnp.stack([ocean_current_east, ocean_current_north]),
            velocity_mask[None],
        ],
        axis=0,
    )
    signs = jnp.array(
        [-1.0, -1.0, 1.0, 1.0, 1.0, 1.0, 1.0, -1.0, -1.0, 1.0], jnp.float32
    ).reshape(-1, 1, 1)
    ext = exchange(stack, width, signs, fold_start, fold_rest)
    grid_row = lax.axis_index("gy") * rows + jnp.arange(-width, rows + width, dtype=jnp.int32)
    true_row = jnp.where(grid_row > total_rows - 1, 2 * total_rows - 1 - grid_row, grid_row)
    coriolis_ext = (FCOR * (true_row.astype(jnp.float32) + 0.5) / float(total_rows))[:, None]
    inside_ext = (grid_row >= 0)[:, None]

    def rows_crop(x, n):
        return x if n == 0 else x[n : x.shape[0] - n]

    vel = ext[0:2]
    st = ext[2:5]
    st_radius = width
    for step in range(ITERS):
        radius = width - 2 * step
        e11, e22, e12 = compute_strain_rates(vel[0], vel[1])
        st = stress_update(
            crop(st, st_radius - (radius - 1)),
            e11,
            e22,
            e12,
            crop(ext[5], width - (radius - 1)),
        )
        st = jnp.where(rows_crop(inside_ext, width - (radius - 1)), st, 0.0)
        st_radius = radius - 1
        eastward_force, northward_force = stress_force(st)
        n = width - (radius - 2)
        vel = momentum_solve(
            crop(vel, 2),
            eastward_force,
            northward_force,
            crop(ext[7:9], n),
            crop(ext[6], n),
            rows_crop(coriolis_ext, n),
            crop(ext[9], n),
        )
        vel = jnp.where(rows_crop(inside_ext, n), vel, 0.0)
    velocity = vel
    stress = crop(st, st_radius)
    thickness_out = column_growth(
        thickness,
        velocity,
        ocean_temp,
        ocean_salt,
        ocean_current_east,
        ocean_current_north,
        air_temp,
        omask,
    )
    return (velocity, stress, thickness_out)


def solution(mesh):
    placed = (
        P("gy", None, "gx"),
        P("gy", "gx"),
        P(None, "gy", "gx"),
        P(None, "gy", "gx"),
        P(None, "gy", "gx"),
        P(None, "gy", "gx"),
        P(None, "gy", "gx"),
        P("gy", "gx"),
        P("gy", "gx"),
        P("gy", "gx"),
        P(),
    )
    return jax.shard_map(
        body,
        mesh=mesh,
        in_specs=placed,
        out_specs=(P(None, "gy", "gx"), P(None, "gy", "gx"), P(None, "gy", "gx")),
        check_vma=False,
    )
```
